256 devices in a mesh: shot: 32 (over y, z_hi, core), depth: 8 (over x, z_lo).
Axes of the slice: x: 4, y: 4, z: 8 (z_hi: 4, z_lo: 2; z = z_hi * 2 + z_lo), core: 2. Of those that a mesh axis runs over, the one named last changes fastest.
Arguments:
- forward_start: bfloat16 [2, 32, 128, 128, 128], P(None, 'shot', 'depth'), may hold values from -6 to 6
- adjoint_end: bfloat16 [2, 32, 128, 128, 128], P(None, 'shot', 'depth'), may hold values from -6 to 6
- velocity: float32 [128, 128, 128], P('depth'), may hold values from 1.5 to 4.5
- source_cell: int32 [32], P('shot'), may hold values from 0 to 2097151
- wavelet: float32 [32, 4], P('shot'), may hold values from -16 to 16
- receiver_cell: int32 [32, 1024], P('shot'), may hold values from 0 to 2097151
- observed: float32 [32, 4, 1024], P('shot'), may hold values from -16 to 16
Outputs:
- forward_end: bfloat16 [2, 32, 128, 128, 128], P(None, 'shot', 'depth')
- adjoint_start: bfloat16 [2, 32, 128, 128, 128], P(None, 'shot', 'depth')
- velocity_new: float32 [128, 128, 128], P('depth')
The draws below stay inside these ranges and needn't reach their ends.
All inputs are finite; a program needn't handle non-finite values.
Results may differ from the reference program's by a relative error of at most 0.0079.
Values may be sent and summed in bfloat16 or wider, within the bound.
No kernel may reach another device: no remote copies, remote signals or barrier semaphores. Data moves between devices by JAX's collectives and lax.ppermute only.
A program may use at most 64 MiB of HBM per device.

```python
import math
import jax
import jax.numpy as jnp
from jax import lax

NX = 128
NY = 128
NREC = 1024
STEPS = 4
NZ = 128
SHOTS = 32


def with_ends(entries, key, smallest, top_value):
    spot = [jax.random.randint(jax.random.fold_in(key, axis), (), 0, length) for axis, length in enumerate(entries.shape)]
    widest = entries.shape.index(max(entries.shape))
    beside = spot[:widest] + [(spot[widest] + 1) % entries.shape[widest]] + spot[widest + 1:]
    return entries.at[tuple(spot)].set(smallest).at[tuple(beside)].set(top_value)


def level_of(key, shape, cuts, smallest, top_value):
    def one(position, parts):
        steps = jax.random.uniform(jax.random.fold_in(jax.random.fold_in(key, 6), position), (parts,), jnp.float32, smallest / len(cuts), top_value / len(cuts))
        return jnp.repeat(jnp.exp(steps), shape[position] // parts).reshape((-1,) + (1,) * (len(shape) - position - 1))

    gain = one(*cuts[0])
    for cut in cuts[1:]:
        gain = gain * one(*cut)
    return gain


def scatter_about(rng, shape, spread, bound, shards=(), held_as=jnp.bfloat16):
    level = level_of(rng, shape, shards, -0.22, 0.18) if shards else 1.0
    drawn = jax.random.normal(rng, shape, jnp.float32) * spread * level
    return jnp.minimum(jnp.maximum(drawn, -bound), bound).astype(held_as)


def setup_inputs(seed: int = 0) -> dict:
    key_list = jax.random.split(jax.random.key(seed), 8)
    forward_start = scatter_about(key_list[0], (2, SHOTS, NZ, NX, NY), 1.0, 6.0, ((1, 32), (2, 8)))
    adjoint_end = scatter_about(key_list[1], (2, SHOTS, NZ, NX, NY), 1.0, 6.0, ((1, 32), (2, 8)))
    velocity = jnp.clip(1.5 + 3.0 * jax.random.uniform(key_list[2], (NZ, NX, NY), jnp.float32) ** level_of(key_list[2], (NZ, NX, NY), ((0, 8),), -0.2, 0.2), 1.5, 4.5)
    source_cell = with_ends(jax.random.randint(key_list[3], (SHOTS,), 0, NZ * NX * NY), jax.random.fold_in(key_list[3], 1), 0, (NZ * NX * NY) - 1).astype(jnp.int32)
    wavelet = scatter_about(key_list[4], (SHOTS, STEPS), 4.0, 16.0, ((0, 32),), jnp.float32)
    receiver_cell = with_ends(jax.random.randint(key_list[5], (SHOTS, NREC), 0, NZ * NX * NY), jax.random.fold_in(key_list[5], 1), 0, (NZ * NX * NY) - 1).astype(jnp.int32)
    observed = scatter_about(key_list[6], (SHOTS, STEPS, NREC), 4.0, 16.0, ((0, 32),), jnp.float32)
    return dict(forward_start=forward_start, adjoint_end=adjoint_end, velocity=velocity, source_cell=source_cell, wavelet=wavelet, receiver_cell=receiver_cell, observed=observed)


stencil_weights = (1.6, -0.2, 8.0 / 315.0, -1.0 / 560.0)
center_weight = -205.0 / 72.0
courant = 0.095
step_base = 0.01
low_speed = 1.5
high_speed = 4.5

def laplace(wavefield):
    padded = jnp.pad(wavefield, 4)
    depth_len, row_len, column_len = wavefield.shape

    def window(along_z, along_x, along_y):
        return padded[4 + along_z:4 + along_z + depth_len, 4 + along_x:4 + along_x + row_len, 4 + along_y:4 + along_y + column_len]
    summed = 3.0 * center_weight * wavefield
    for offset in range(1, 5):
        weight = stencil_weights[offset - 1]
        summed = summed + weight * (window(offset, 0, 0) + window(-offset, 0, 0) + window(0, offset, 0) + window(0, -offset, 0) + window(0, 0, offset) + window(0, 0, -offset))
    return summed

def reference(forward_start, adjoint_end, velocity, source_cell, wavelet, receiver_cell, observed):
    wave_model = (courant * velocity) ** 2
    grid_shape = velocity.shape

    def per_shot(gradient, inputs):
        start_pair, end_pair, source_id, pulse, receiver_ids, recorded = inputs
        earlier = start_pair[0]
        current = start_pair[1]
        images = []
        residuals = []
        for moment in range(STEPS):
            laplacian = laplace(current.astype(jnp.float32))
            updated = 2.0 * current.astype(jnp.float32) - earlier.astype(jnp.float32) + wave_model * laplacian
            updated = updated.reshape(-1).at[source_id].add(pulse[moment]).reshape(grid_shape).astype(jnp.bfloat16)
            images.append(laplacian.astype(jnp.bfloat16))
            synthetic = updated.reshape(-1)[receiver_ids].astype(jnp.float32)
            residuals.append(synthetic - recorded[moment])
            earlier, current = (current, updated)
        images = list(lax.optimization_barrier(tuple(images)))
        nearer = end_pair[0]
        farther = end_pair[1]
        shot_gradient = jnp.zeros(grid_shape, jnp.float32)
        for moment in reversed(range(STEPS)):
            laplacian = laplace(nearer.astype(jnp.float32))
            updated = 2.0 * nearer.astype(jnp.float32) - farther.astype(jnp.float32) + wave_model * laplacian
            updated = updated.reshape(-1).at[receiver_ids].add(residuals[moment]).reshape(grid_shape).astype(jnp.bfloat16)
            shot_gradient = shot_gradient + updated.astype(jnp.float32) * images[moment].astype(jnp.float32)
            farther, nearer = (nearer, updated)
        forward_pair = jnp.stack([earlier, current])
        adjoint_pair = jnp.stack([nearer, farther])
        return (gradient + shot_gradient, (forward_pair, adjoint_pair))
    inputs = (jnp.moveaxis(forward_start, 1, 0), jnp.moveaxis(adjoint_end, 1, 0), source_cell, wavelet, receiver_cell, observed)
    gradient, (forward_pairs, adjoint_pairs) = lax.scan(per_shot, jnp.zeros(grid_shape, jnp.float32), inputs)
    step_scale = step_base / math.sqrt(SHOTS)
    velocity_new = jnp.clip(velocity - step_scale * gradient, low_speed, high_speed)
    return (jnp.moveaxis(forward_pairs, 0, 1), jnp.moveaxis(adjoint_pairs, 0, 1), velocity_new)
```

```python
import math

import jax
import jax.numpy as jnp
from jax import lax
from jax.sharding import Mesh
from jax.sharding import PartitionSpec as P

SHOT = ("y", "zhi", "core")
DEPTH = ("x", "zlo")
CZ = 16
NX = 128
NY = 128
STEPS = 4


stencil_weights = (1.6, -0.2, 8.0 / 315.0, -1.0 / 560.0)
center_weight = -205.0 / 72.0
courant = 0.095
step_base = 0.01
low_speed = 1.5
high_speed = 4.5


def padded_2(cells, sides, width):
    for axis, dim in sides:
        count = lax.axis_size(axis)
        ends = count - 1
        head = lax.slice_in_dim(cells, 0, width, axis=dim)
        tail = lax.slice_in_dim(cells, cells.shape[dim] - width, cells.shape[dim], axis=dim)
        cells = jnp.concatenate(
            [
                lax.ppermute(tail, axis, [(i, (i + 1) % count) for i in range(ends)]),
                cells,
                lax.ppermute(head, axis, [((i + 1) % count, i) for i in range(ends)]),
            ],
            axis=dim,
        )
    return cells


def laplace(depth_padded):
    padded = jnp.pad(depth_padded, ((0, 0), (0, 0), (4, 4), (4, 4)))
    depth_len = padded.shape[1] - 8
    row_len = padded.shape[2] - 8
    column_len = padded.shape[3] - 8

    def window(along_z, along_x, along_y):
        return padded[
            :,
            4 + along_z : 4 + along_z + depth_len,
            4 + along_x : 4 + along_x + row_len,
            4 + along_y : 4 + along_y + column_len,
        ]

    summed = 3.0 * center_weight * window(0, 0, 0)
    for offset in range(1, 5):
        weight = stencil_weights[offset - 1]
        summed = summed + weight * (
            window(offset, 0, 0)
            + window(-offset, 0, 0)
            + window(0, offset, 0)
            + window(0, -offset, 0)
            + window(0, 0, offset)
            + window(0, 0, -offset)
        )
    return summed


def inject(wavefield, cell_ids, values, anchor):
    shot_count = wavefield.shape[0]
    depth_len = wavefield.shape[1]
    plane_size = NX * NY
    planes = cell_ids // plane_size - anchor
    owned_mask = (planes >= 0) & (planes < depth_len)
    flat_index = jnp.clip(planes, 0, depth_len - 1) * plane_size + cell_ids % plane_size
    rows_index = jnp.broadcast_to(jnp.arange(shot_count, dtype=jnp.int32)[:, None], cell_ids.shape)
    flattened = (
        wavefield.reshape(shot_count, -1)
        .at[rows_index, flat_index]
        .add(jnp.where(owned_mask, values, 0.0))
    )
    return flattened.reshape(wavefield.shape)


def cell_coords(cell_ids, anchor):
    plane_size = NX * NY
    planes = cell_ids // plane_size - anchor
    rest = cell_ids % plane_size
    return planes, rest // NY, rest % NY


def inject_one(wavefield, cell_ids, values, anchor):
    planes, rows, columns = cell_coords(cell_ids, anchor)
    shape = wavefield.shape
    hit = (
        (lax.broadcasted_iota(jnp.int32, shape, 1) == planes[:, None, None, None])
        & (lax.broadcasted_iota(jnp.int32, shape, 2) == rows[:, None, None, None])
        & (lax.broadcasted_iota(jnp.int32, shape, 3) == columns[:, None, None, None])
    )
    return jnp.where(hit, wavefield + values[:, :, None, None], wavefield)


def record_rows(wavefield, cell_ids, anchor):
    depth_len = wavefield.shape[1]
    planes, rows, columns = cell_coords(cell_ids, anchor)
    row_ids = jnp.clip(planes, 0, depth_len - 1) * NX + rows
    table = wavefield.reshape(-1, NY)
    picked = table[row_ids[0]].astype(jnp.float32)
    lanes = lax.broadcasted_iota(jnp.int32, picked.shape, 1)
    return jnp.sum(jnp.where(lanes == columns[0][:, None], picked, 0.0), axis=1)[None]


def record(wavefield, cell_ids, anchor):
    shot_count = wavefield.shape[0]
    plane_size = NX * NY
    planes = cell_ids // plane_size - anchor
    flat_index = jnp.clip(planes, 0, wavefield.shape[1] - 1) * plane_size + cell_ids % plane_size
    return jnp.take_along_axis(wavefield.reshape(shot_count, -1), flat_index, axis=1).astype(
        jnp.float32
    )


HALVINGS = (("core", 1), ("zhi", 1), ("zhi", 2), ("y", 1), ("y", 2))


def partner_bit(axis, mask):
    count = lax.axis_size(axis)
    bit = (lax.axis_index(axis) // mask) % 2
    return bit, [(i, i ^ mask) for i in range(count)]


def reduce_shots(gradient):
    rows = gradient.reshape(-1, gradient.shape[-1])
    for axis, mask in HALVINGS:
        bit, perm = partner_bit(axis, mask)
        half = rows.shape[0] // 2
        keep = lax.dynamic_slice_in_dim(rows, bit * half, half, 0)
        send = lax.dynamic_slice_in_dim(rows, (1 - bit) * half, half, 0)
        rows = keep + lax.ppermute(send, axis, perm)
    for axis, mask in reversed(HALVINGS):
        bit, perm = partner_bit(axis, mask)
        other = lax.ppermute(rows, axis, perm)
        rows = jnp.where(
            bit == 0, jnp.concatenate([rows, other]), jnp.concatenate([other, rows])
        )
    return rows.reshape(gradient.shape)


def body(forward_start, adjoint_end, velocity, source_cell, wavelet, receiver_cell, observed):
    anchor = lax.axis_index(DEPTH) * CZ
    wave_model = (courant * velocity) ** 2
    source_ids = source_cell[:, None]
    images = []
    residuals = []
    earlier = forward_start[0]
    current = forward_start[1]
    for moment in range(STEPS):
        padded = padded_2(current, ((DEPTH, 1),), 4)
        laplacian = laplace(padded.astype(jnp.float32))
        updated = (
            2.0 * current.astype(jnp.float32) - earlier.astype(jnp.float32) + wave_model * laplacian
        )
        updated = inject_one(updated, source_cell, wavelet[:, moment : moment + 1], anchor).astype(
            jnp.bfloat16
        )
        images.append(laplacian.astype(jnp.bfloat16))
        residuals.append(record_rows(updated, receiver_cell, anchor) - observed[:, moment])
        earlier, current = (current, updated)
    images = list(lax.optimization_barrier(tuple(images)))
    nearer = adjoint_end[0]
    farther = adjoint_end[1]
    gradient = jnp.zeros(velocity.shape, jnp.float32)
    for moment in reversed(range(STEPS)):
        padded = padded_2(nearer, ((DEPTH, 1),), 4)
        laplacian = laplace(padded.astype(jnp.float32))
        updated = (
            2.0 * nearer.astype(jnp.float32) - farther.astype(jnp.float32) + wave_model * laplacian
        )
        updated = inject(updated, receiver_cell, residuals[moment], anchor).astype(jnp.bfloat16)
        gradient = gradient + jnp.sum(
            updated.astype(jnp.float32) * images[moment].astype(jnp.float32), axis=0
        )
        farther, nearer = (nearer, updated)
    step_scale = step_base / math.sqrt(forward_start.shape[1] * lax.axis_size(SHOT))
    summed = reduce_shots(gradient)
    velocity_new = jnp.clip(velocity - step_scale * summed, low_speed, high_speed)
    forward_end = jnp.stack([earlier, current])
    adjoint_start = jnp.stack([nearer, farther])
    return (forward_end, adjoint_start, velocity_new)


def solution(mesh):
    fine = Mesh(mesh.devices.reshape(4, 4, 2, 4, 2), ("y", "zhi", "core", "x", "zlo"))
    placed = (
        P(None, SHOT, DEPTH, None, None),
        P(None, SHOT, DEPTH, None, None),
        P(DEPTH, None, None),
        P(SHOT),
        P(SHOT, None),
        P(SHOT, None),
        P(SHOT, None, None),
    )
    return jax.shard_map(
        body,
        mesh=fine,
        in_specs=placed,
        out_specs=(
            P(None, SHOT, DEPTH, None, None),
            P(None, SHOT, DEPTH, None, None),
            P(DEPTH, None, None),
        ),
        check_vma=False,
    )
```

```python
import math

import jax
import jax.numpy as jnp
from jax import lax
from jax.sharding import Mesh
from jax.sharding import PartitionSpec as P

SHOT = ("y", "zhi", "core")
DEPTH = ("x", "zlo")
CZ = 16
NX = 128
NY = 128
STEPS = 4


stencil_weights = (1.6, -0.2, 8.0 / 315.0, -1.0 / 560.0)
center_weight = -205.0 / 72.0
courant = 0.095
step_base = 0.01
low_speed = 1.5
high_speed = 4.5


def padded_2(cells, sides, width):
    for axis, dim in sides:
        count = lax.axis_size(axis)
        ends = count - 1
        head = lax.slice_in_dim(cells, 0, width, axis=dim)
        tail = lax.slice_in_dim(cells, cells.shape[dim] - width, cells.shape[dim], axis=dim)
        cells = jnp.concatenate(
            [
                lax.ppermute(tail, axis, [(i, (i + 1) % count) for i in range(ends)]),
                cells,
                lax.ppermute(head, axis, [((i + 1) % count, i) for i in range(ends)]),
            ],
            axis=dim,
        )
    return cells


def laplace(depth_padded):
    padded = jnp.pad(depth_padded, ((0, 0), (0, 0), (4, 4), (4, 4)))
    depth_len = padded.shape[1] - 8
    row_len = padded.shape[2] - 8
    column_len = padded.shape[3] - 8

    def window(along_z, along_x, along_y):
        return padded[
            :,
            4 + along_z : 4 + along_z + depth_len,
            4 + along_x : 4 + along_x + row_len,
            4 + along_y : 4 + along_y + column_len,
        ]

    summed = 3.0 * center_weight * window(0, 0, 0)
    for offset in range(1, 5):
        weight = stencil_weights[offset - 1]
        summed = summed + weight * (
            window(offset, 0, 0)
            + window(-offset, 0, 0)
            + window(0, offset, 0)
            + window(0, -offset, 0)
            + window(0, 0, offset)
            + window(0, 0, -offset)
        )
    return summed


def inject(wavefield, cell_ids, values, anchor):
    shot_count = wavefield.shape[0]
    depth_len = wavefield.shape[1]
    plane_size = NX * NY
    planes = cell_ids // plane_size - anchor
    owned_mask = (planes >= 0) & (planes < depth_len)
    flat_index = jnp.clip(planes, 0, depth_len - 1) * plane_size + cell_ids % plane_size
    rows_index = jnp.broadcast_to(jnp.arange(shot_count, dtype=jnp.int32)[:, None], cell_ids.shape)
    flattened = (
        wavefield.reshape(shot_count, -1)
        .at[rows_index, flat_index]
        .add(jnp.where(owned_mask, values, 0.0))
    )
    return flattened.reshape(wavefield.shape)


def cell_coords(cell_ids, anchor):
    plane_size = NX * NY
    planes = cell_ids // plane_size - anchor
    rest = cell_ids % plane_size
    return planes, rest // NY, rest % NY


def inject_one(wavefield, cell_ids, values, anchor):
    planes, rows, columns = cell_coords(cell_ids, anchor)
    shape = wavefield.shape
    hit = (
        (lax.broadcasted_iota(jnp.int32, shape, 1) == planes[:, None, None, None])
        & (lax.broadcasted_iota(jnp.int32, shape, 2) == rows[:, None, None, None])
        & (lax.broadcasted_iota(jnp.int32, shape, 3) == columns[:, None, None, None])
    )
    return jnp.where(hit, wavefield + values[:, :, None, None], wavefield)


def record_rows(wavefield, cell_ids, anchor):
    depth_len = wavefield.shape[1]
    planes, rows, columns = cell_coords(cell_ids, anchor)
    row_ids = jnp.clip(planes, 0, depth_len - 1) * NX + rows
    table = wavefield.reshape(-1, NY)
    picked = table[row_ids[0]].astype(jnp.float32)
    lanes = lax.broadcasted_iota(jnp.int32, picked.shape, 1)
    return jnp.sum(jnp.where(lanes == columns[0][:, None], picked, 0.0), axis=1)[None]


def record(wavefield, cell_ids, anchor):
    shot_count = wavefield.shape[0]
    plane_size = NX * NY
    planes = cell_ids // plane_size - anchor
    flat_index = jnp.clip(planes, 0, wavefield.shape[1] - 1) * plane_size + cell_ids % plane_size
    return jnp.take_along_axis(wavefield.reshape(shot_count, -1), flat_index, axis=1).astype(
        jnp.float32
    )


HALVINGS = (("core", 1), ("zhi", 1), ("zhi", 2), ("y", 1), ("y", 2))


def partner_bit(axis, mask):
    count = lax.axis_size(axis)
    bit = (lax.axis_index(axis) // mask) % 2
    return bit, [(i, i ^ mask) for i in range(count)]


def reduce_shots(gradient):
    rows = gradient.reshape(-1, gradient.shape[-1])
    for axis, mask in HALVINGS:
        bit, perm = partner_bit(axis, mask)
        half = rows.shape[0] // 2
        keep = lax.dynamic_slice_in_dim(rows, bit * half, half, 0)
        send = lax.dynamic_slice_in_dim(rows, (1 - bit) * half, half, 0)
        rows = keep + lax.ppermute(send, axis, perm)
    for axis, mask in reversed(HALVINGS):
        bit, perm = partner_bit(axis, mask)
        other = lax.ppermute(rows, axis, perm)
        rows = jnp.where(
            bit == 0, jnp.concatenate([rows, other]), jnp.concatenate([other, rows])
        )
    return rows.reshape(gradient.shape)


def edges(cells, width):
    count = lax.axis_size(DEPTH)
    below = lax.ppermute(cells[:, -width:], DEPTH, [(i, i + 1) for i in range(count - 1)])
    above = lax.ppermute(cells[:, :width], DEPTH, [(i + 1, i) for i in range(count - 1)])
    return below, above


def around(cells, below, above, width):
    depth = below.shape[1]
    return jnp.concatenate(
        [below[:, depth - width :], cells, above[:, :width]], axis=1
    )


def leap(current, earlier, model, stencil, extra):
    updated = 2.0 * current.astype(jnp.float32) - earlier.astype(jnp.float32) + model * stencil
    return updated + extra


def body(forward_start, adjoint_end, velocity, source_cell, wavelet, receiver_cell, observed):
    depth_len = velocity.shape[0]
    anchor = lax.axis_index(DEPTH) * depth_len
    wide = anchor - 4
    wave_model = ((courant * velocity) ** 2)[None]
    model_below, model_above = edges(wave_model, 4)
    model_wide = around(wave_model, model_below, model_above, 4)
    zeros_own = jnp.zeros(forward_start.shape[1:], jnp.float32)
    zeros_wide = jnp.zeros(model_wide.shape, jnp.float32)

    def source(moment, zeros, base):
        return inject_one(zeros, source_cell, wavelet[:, moment : moment + 1], base)

    first, second = forward_start[0], forward_start[1]
    pair_below, pair_above = edges(
        jnp.concatenate([first[:, :4], second[:, :8], first[:, -4:], second[:, -8:]], axis=1), 12
    )
    images = []
    residuals = []
    second_pad = jnp.concatenate([pair_below[:, 4:12], second, pair_above[:, 4:12]], axis=1)
    first_wide = jnp.concatenate([pair_below[:, 0:4], first, pair_above[:, 0:4]], axis=1)
    stencil = laplace(second_pad.astype(jnp.float32))
    wide_next = leap(second_pad[:, 4:-4], first_wide, model_wide, stencil, source(0, zeros_wide, wide)).astype(jnp.bfloat16)
    images.append(stencil[:, 4:-4].astype(jnp.bfloat16))
    residuals.append(record_rows(wide_next, receiver_cell, wide) - observed[:, 0])
    stencil = laplace(wide_next.astype(jnp.float32))
    own_next = leap(wide_next[:, 4:-4], second, wave_model, stencil, source(1, zeros_own, anchor)).astype(jnp.bfloat16)
    images.append(stencil.astype(jnp.bfloat16))
    residuals.append(record_rows(own_next, receiver_cell, anchor) - observed[:, 1])
    below, above = edges(own_next, 8)
    third_pad = around(own_next, below, above, 8)
    stencil = laplace(third_pad.astype(jnp.float32))
    wide_four = leap(third_pad[:, 4:-4], wide_next, model_wide, stencil, source(2, zeros_wide, wide)).astype(jnp.bfloat16)
    images.append(stencil[:, 4:-4].astype(jnp.bfloat16))
    residuals.append(record_rows(wide_four, receiver_cell, wide) - observed[:, 2])
    stencil = laplace(wide_four.astype(jnp.float32))
    own_five = leap(wide_four[:, 4:-4], own_next, wave_model, stencil, source(3, zeros_own, anchor)).astype(jnp.bfloat16)
    images.append(stencil.astype(jnp.bfloat16))
    residuals.append(record_rows(own_five, receiver_cell, anchor) - observed[:, 3])
    forward_end = jnp.stack([wide_four[:, 4:-4], own_five])
    images = list(lax.optimization_barrier(tuple(images)))

    injected = [
        inject(zeros_own, receiver_cell, residuals[0], anchor),
        inject(zeros_own, receiver_cell, residuals[1], anchor),
        inject(zeros_wide, receiver_cell, residuals[2], wide),
        inject(zeros_own, receiver_cell, residuals[3], anchor),
    ]
    nearer, farther = adjoint_end[0], adjoint_end[1]
    below, above = edges(nearer, 4)
    five_pad = around(nearer, below, above, 4)
    stencil = laplace(five_pad.astype(jnp.float32))
    q4 = leap(nearer, farther, wave_model, stencil, injected[3]).astype(jnp.bfloat16)
    below, above = edges(q4, 8)
    four_pad = around(q4, below, above, 8)
    stencil = laplace(four_pad.astype(jnp.float32))
    q3_wide = leap(four_pad[:, 4:-4], five_pad, model_wide, stencil, injected[2]).astype(jnp.bfloat16)
    stencil = laplace(q3_wide.astype(jnp.float32))
    q2 = leap(q3_wide[:, 4:-4], q4, wave_model, stencil, injected[1]).astype(jnp.bfloat16)
    below, above = edges(q2, 4)
    two_pad = around(q2, below, above, 4)
    stencil = laplace(two_pad.astype(jnp.float32))
    q1 = leap(q2, q3_wide[:, 4:-4], wave_model, stencil, injected[0]).astype(jnp.bfloat16)

    gradient = jnp.zeros(velocity.shape, jnp.float32)
    for field, image in ((q4, images[3]), (q3_wide[:, 4:-4], images[2]), (q2, images[1]), (q1, images[0])):
        gradient = gradient + jnp.sum(field.astype(jnp.float32) * image.astype(jnp.float32), axis=0)
    step_scale = step_base / math.sqrt(forward_start.shape[1] * lax.axis_size(SHOT))
    summed = reduce_shots(gradient)
    velocity_new = jnp.clip(velocity - step_scale * summed, low_speed, high_speed)
    adjoint_start = jnp.stack([q1, q2])
    return (forward_end, adjoint_start, velocity_new)


def solution(mesh):
    fine = Mesh(mesh.devices.reshape(4, 4, 2, 4, 2), ("y", "zhi", "core", "x", "zlo"))
    placed = (
        P(None, SHOT, DEPTH, None, None),
        P(None, SHOT, DEPTH, None, None),
        P(DEPTH, None, None),
        P(SHOT),
        P(SHOT, None),
        P(SHOT, None),
        P(SHOT, None, None),
    )
    return jax.shard_map(
        body,
        mesh=fine,
        in_specs=placed,
        out_specs=(
            P(None, SHOT, DEPTH, None, None),
            P(None, SHOT, DEPTH, None, None),
            P(DEPTH, None, None),
        ),
        check_vma=False,
    )
```

```python
import math

import jax
import jax.numpy as jnp
from jax import lax
from jax.sharding import Mesh
from jax.sharding import PartitionSpec as P

SHOT = ("y", "zhi", "core")
DEPTH = ("x", "zlo")
CZ = 16
NX = 128
NY = 128
STEPS = 4


stencil_weights = (1.6, -0.2, 8.0 / 315.0, -1.0 / 560.0)
center_weight = -205.0 / 72.0
courant = 0.095
step_base = 0.01
low_speed = 1.5
high_speed = 4.5


def padded_2(cells, sides, width):
    for axis, dim in sides:
        count = lax.axis_size(axis)
        ends = count - 1
        head = lax.slice_in_dim(cells, 0, width, axis=dim)
        tail = lax.slice_in_dim(cells, cells.shape[dim] - width, cells.shape[dim], axis=dim)
        cells = jnp.concatenate(
            [
                lax.ppermute(tail, axis, [(i, (i + 1) % count) for i in range(ends)]),
                cells,
                lax.ppermute(head, axis, [((i + 1) % count, i) for i in range(ends)]),
            ],
            axis=dim,
        )
    return cells


def laplace(depth_padded):
    padded = jnp.pad(depth_padded, ((0, 0), (0, 0), (4, 4), (4, 4)))
    depth_len = padded.shape[1] - 8
    row_len = padded.shape[2] - 8
    column_len = padded.shape[3] - 8

    def window(along_z, along_x, along_y):
        return padded[
            :,
            4 + along_z : 4 + along_z + depth_len,
            4 + along_x : 4 + along_x + row_len,
            4 + along_y : 4 + along_y + column_len,
        ]

    summed = 3.0 * center_weight * window(0, 0, 0)
    for offset in range(1, 5):
        weight = stencil_weights[offset - 1]
        summed = summed + weight * (
            window(offset, 0, 0)
            + window(-offset, 0, 0)
            + window(0, offset, 0)
            + window(0, -offset, 0)
            + window(0, 0, offset)
            + window(0, 0, -offset)
        )
    return summed


def inject(wavefield, cell_ids, values, anchor):
    shot_count = wavefield.shape[0]
    depth_len = wavefield.shape[1]
    plane_size = NX * NY
    planes = cell_ids // plane_size - anchor
    owned_mask = (planes >= 0) & (planes < depth_len)
    flat_index = jnp.clip(planes, 0, depth_len - 1) * plane_size + cell_ids % plane_size
    rows_index = jnp.broadcast_to(jnp.arange(shot_count, dtype=jnp.int32)[:, None], cell_ids.shape)
    flattened = (
        wavefield.reshape(shot_count, -1)
        .at[rows_index, flat_index]
        .add(jnp.where(owned_mask, values, 0.0))
    )
    return flattened.reshape(wavefield.shape)


def cell_coords(cell_ids, anchor):
    plane_size = NX * NY
    planes = cell_ids // plane_size - anchor
    rest = cell_ids % plane_size
    return planes, rest // NY, rest % NY


def inject_one(wavefield, cell_ids, values, anchor):
    planes, rows, columns = cell_coords(cell_ids, anchor)
    shape = wavefield.shape
    hit = (
        (lax.broadcasted_iota(jnp.int32, shape, 1) == planes[:, None, None, None])
        & (lax.broadcasted_iota(jnp.int32, shape, 2) == rows[:, None, None, None])
        & (lax.broadcasted_iota(jnp.int32, shape, 3) == columns[:, None, None, None])
    )
    return jnp.where(hit, wavefield + values[:, :, None, None], wavefield)


def record_rows(wavefield, cell_ids, anchor):
    depth_len = wavefield.shape[1]
    planes, rows, columns = cell_coords(cell_ids, anchor)
    row_ids = jnp.clip(planes, 0, depth_len - 1) * NX + rows
    table = wavefield.reshape(-1, NY)
    picked = table[row_ids[0]].astype(jnp.float32)
    lanes = lax.broadcasted_iota(jnp.int32, picked.shape, 1)
    return jnp.sum(jnp.where(lanes == columns[0][:, None], picked, 0.0), axis=1)[None]


def record(wavefield, cell_ids, anchor):
    shot_count = wavefield.shape[0]
    plane_size = NX * NY
    planes = cell_ids // plane_size - anchor
    flat_index = jnp.clip(planes, 0, wavefield.shape[1] - 1) * plane_size + cell_ids % plane_size
    return jnp.take_along_axis(wavefield.reshape(shot_count, -1), flat_index, axis=1).astype(
        jnp.float32
    )


HALVINGS = (("core", 1), ("y", 1), ("y", 2), ("zhi", 1), ("zhi", 2))


def partner_bit(axis, mask):
    count = lax.axis_size(axis)
    bit = (lax.axis_index(axis) // mask) % 2
    return bit, [(i, i ^ mask) for i in range(count)]


def reduce_shots(gradient):
    rows = gradient.reshape(-1, gradient.shape[-1])
    for axis, mask in HALVINGS:
        bit, perm = partner_bit(axis, mask)
        half = rows.shape[0] // 2
        keep = lax.dynamic_slice_in_dim(rows, bit * half, half, 0)
        send = lax.dynamic_slice_in_dim(rows, (1 - bit) * half, half, 0)
        rows = keep + lax.ppermute(send, axis, perm)
    for axis, mask in reversed(HALVINGS):
        bit, perm = partner_bit(axis, mask)
        other = lax.ppermute(rows, axis, perm)
        rows = jnp.where(
            bit == 0, jnp.concatenate([rows, other]), jnp.concatenate([other, rows])
        )
    return rows.reshape(gradient.shape)


def body(forward_start, adjoint_end, velocity, source_cell, wavelet, receiver_cell, observed):
    anchor = lax.axis_index(DEPTH) * CZ
    wave_model = (courant * velocity) ** 2
    source_ids = source_cell[:, None]
    images = []
    residuals = []
    earlier = forward_start[0]
    current = forward_start[1]
    for moment in range(STEPS):
        padded = padded_2(current, ((DEPTH, 1),), 4)
        laplacian = laplace(padded.astype(jnp.float32))
        updated = (
            2.0 * current.astype(jnp.float32) - earlier.astype(jnp.float32) + wave_model * laplacian
        )
        updated = inject_one(updated, source_cell, wavelet[:, moment : moment + 1], anchor).astype(
            jnp.bfloat16
        )
        images.append(laplacian.astype(jnp.bfloat16))
        residuals.append(record_rows(updated, receiver_cell, anchor) - observed[:, moment])
        earlier, current = (current, updated)
    images = list(lax.optimization_barrier(tuple(images)))
    nearer = adjoint_end[0]
    farther = adjoint_end[1]
    gradient = jnp.zeros(velocity.shape, jnp.float32)
    for moment in reversed(range(STEPS)):
        padded = padded_2(nearer, ((DEPTH, 1),), 4)
        laplacian = laplace(padded.astype(jnp.float32))
        updated = (
            2.0 * nearer.astype(jnp.float32) - farther.astype(jnp.float32) + wave_model * laplacian
        )
        updated = inject(updated, receiver_cell, residuals[moment], anchor).astype(jnp.bfloat16)
        gradient = gradient + jnp.sum(
            updated.astype(jnp.float32) * images[moment].astype(jnp.float32), axis=0
        )
        farther, nearer = (nearer, updated)
    step_scale = step_base / math.sqrt(forward_start.shape[1] * lax.axis_size(SHOT))
    summed = reduce_shots(gradient)
    velocity_new = jnp.clip(velocity - step_scale * summed, low_speed, high_speed)
    forward_end = jnp.stack([earlier, current])
    adjoint_start = jnp.stack([nearer, farther])
    return (forward_end, adjoint_start, velocity_new)


def solution(mesh):
    fine = Mesh(mesh.devices.reshape(4, 4, 2, 4, 2), ("y", "zhi", "core", "x", "zlo"))
    placed = (
        P(None, SHOT, DEPTH, None, None),
        P(None, SHOT, DEPTH, None, None),
        P(DEPTH, None, None),
        P(SHOT),
        P(SHOT, None),
        P(SHOT, None),
        P(SHOT, None, None),
    )
    return jax.shard_map(
        body,
        mesh=fine,
        in_specs=placed,
        out_specs=(
            P(None, SHOT, DEPTH, None, None),
            P(None, SHOT, DEPTH, None, None),
            P(DEPTH, None, None),
        ),
        check_vma=False,
    )
```

```python
import math

import jax
import jax.numpy as jnp
from jax import lax
from jax.sharding import Mesh
from jax.sharding import PartitionSpec as P

SHOT = ("y", "zhi", "core")
DEPTH = ("x", "zlo")
CZ = 16
NX = 128
NY = 128
STEPS = 4


stencil_weights = (1.6, -0.2, 8.0 / 315.0, -1.0 / 560.0)
center_weight = -205.0 / 72.0
courant = 0.095
step_base = 0.01
low_speed = 1.5
high_speed = 4.5


def padded_2(cells, sides, width):
    for axis, dim in sides:
        count = lax.axis_size(axis)
        ends = count - 1
        head = lax.slice_in_dim(cells, 0, width, axis=dim)
        tail = lax.slice_in_dim(cells, cells.shape[dim] - width, cells.shape[dim], axis=dim)
        cells = jnp.concatenate(
            [
                lax.ppermute(tail, axis, [(i, (i + 1) % count) for i in range(ends)]),
                cells,
                lax.ppermute(head, axis, [((i + 1) % count, i) for i in range(ends)]),
            ],
            axis=dim,
        )
    return cells


def laplace(depth_padded):
    padded = jnp.pad(depth_padded, ((0, 0), (0, 0), (4, 4), (4, 4)))
    depth_len = padded.shape[1] - 8
    row_len = padded.shape[2] - 8
    column_len = padded.shape[3] - 8

    def window(along_z, along_x, along_y):
        return padded[
            :,
            4 + along_z : 4 + along_z + depth_len,
            4 + along_x : 4 + along_x + row_len,
            4 + along_y : 4 + along_y + column_len,
        ]

    summed = 3.0 * center_weight * window(0, 0, 0)
    for offset in range(1, 5):
        weight = stencil_weights[offset - 1]
        summed = summed + weight * (
            window(offset, 0, 0)
            + window(-offset, 0, 0)
            + window(0, offset, 0)
            + window(0, -offset, 0)
            + window(0, 0, offset)
            + window(0, 0, -offset)
        )
    return summed


def inject(wavefield, cell_ids, values, anchor):
    shot_count = wavefield.shape[0]
    depth_len = wavefield.shape[1]
    plane_size = NX * NY
    planes = cell_ids // plane_size - anchor
    owned_mask = (planes >= 0) & (planes < depth_len)
    flat_index = jnp.clip(planes, 0, depth_len - 1) * plane_size + cell_ids % plane_size
    rows_index = jnp.broadcast_to(jnp.arange(shot_count, dtype=jnp.int32)[:, None], cell_ids.shape)
    flattened = (
        wavefield.reshape(shot_count, -1)
        .at[rows_index, flat_index]
        .add(jnp.where(owned_mask, values, 0.0))
    )
    return flattened.reshape(wavefield.shape)


def cell_coords(cell_ids, anchor):
    plane_size = NX * NY
    planes = cell_ids // plane_size - anchor
    rest = cell_ids % plane_size
    return planes, rest // NY, rest % NY


def inject_one(wavefield, cell_ids, values, anchor):
    planes, rows, columns = cell_coords(cell_ids, anchor)
    shape = wavefield.shape
    hit = (
        (lax.broadcasted_iota(jnp.int32, shape, 1) == planes[:, None, None, None])
        & (lax.broadcasted_iota(jnp.int32, shape, 2) == rows[:, None, None, None])
        & (lax.broadcasted_iota(jnp.int32, shape, 3) == columns[:, None, None, None])
    )
    return jnp.where(hit, wavefield + values[:, :, None, None], wavefield)


def record_rows(wavefield, cell_ids, anchor):
    depth_len = wavefield.shape[1]
    planes, rows, columns = cell_coords(cell_ids, anchor)
    row_ids = jnp.clip(planes, 0, depth_len - 1) * NX + rows
    table = wavefield.reshape(-1, NY)
    choose = row_ids[0][:, None] == lax.broadcasted_iota(jnp.int32, (1, table.shape[0]), 1)
    picked = jnp.dot(choose.astype(table.dtype), table, preferred_element_type=jnp.float32)
    lanes = lax.broadcasted_iota(jnp.int32, picked.shape, 1)
    return jnp.sum(jnp.where(lanes == columns[0][:, None], picked, 0.0), axis=1)[None]


def inject_rows(wavefield, cell_ids, values, anchor):
    depth_len = wavefield.shape[1]
    planes, rows, columns = cell_coords(cell_ids, anchor)
    owned = (planes >= 0) & (planes < depth_len)
    row_ids = jnp.clip(planes, 0, depth_len - 1) * NX + rows
    count = depth_len * NX
    choose = row_ids[0][:, None] == lax.broadcasted_iota(jnp.int32, (1, count), 1)
    lanes = lax.broadcasted_iota(jnp.int32, (cell_ids.shape[1], NY), 1)
    spread = jnp.where(
        (lanes == columns[0][:, None]) & owned[0][:, None], values[0][:, None], 0.0
    )
    high = lax.reduce_precision(spread, exponent_bits=8, mantissa_bits=7)
    rest = spread - high
    middle = lax.reduce_precision(rest, exponent_bits=8, mantissa_bits=7)
    low = rest - middle
    pieces = jnp.concatenate([high, middle, low], axis=1).astype(jnp.bfloat16)
    parts = lax.dot_general(
        choose.astype(jnp.bfloat16),
        pieces,
        (((0,), (0,)), ((), ())),
        preferred_element_type=jnp.float32,
    )
    added = (parts[:, :NY] + parts[:, NY : 2 * NY]) + parts[:, 2 * NY :]
    return wavefield + added.reshape(wavefield.shape)


def record(wavefield, cell_ids, anchor):
    shot_count = wavefield.shape[0]
    plane_size = NX * NY
    planes = cell_ids // plane_size - anchor
    flat_index = jnp.clip(planes, 0, wavefield.shape[1] - 1) * plane_size + cell_ids % plane_size
    return jnp.take_along_axis(wavefield.reshape(shot_count, -1), flat_index, axis=1).astype(
        jnp.float32
    )


HALVINGS = (("core", 1), ("y", 1), ("y", 2), ("zhi", 1), ("zhi", 2))


def partner_bit(axis, mask):
    count = lax.axis_size(axis)
    bit = (lax.axis_index(axis) // mask) % 2
    return bit, [(i, i ^ mask) for i in range(count)]


def reduce_shots(gradient):
    rows = gradient.reshape(-1, gradient.shape[-1])
    for axis, mask in HALVINGS:
        bit, perm = partner_bit(axis, mask)
        half = rows.shape[0] // 2
        keep = lax.dynamic_slice_in_dim(rows, bit * half, half, 0)
        send = lax.dynamic_slice_in_dim(rows, (1 - bit) * half, half, 0)
        rows = keep + lax.ppermute(send, axis, perm)
    for axis, mask in reversed(HALVINGS):
        bit, perm = partner_bit(axis, mask)
        other = lax.ppermute(rows, axis, perm)
        rows = jnp.where(
            bit == 0, jnp.concatenate([rows, other]), jnp.concatenate([other, rows])
        )
    return rows.reshape(gradient.shape)


def body(forward_start, adjoint_end, velocity, source_cell, wavelet, receiver_cell, observed):
    anchor = lax.axis_index(DEPTH) * CZ
    wave_model = (courant * velocity) ** 2
    source_ids = source_cell[:, None]
    images = []
    residuals = []
    earlier = forward_start[0]
    current = forward_start[1]
    for moment in range(STEPS):
        padded = padded_2(current, ((DEPTH, 1),), 4)
        laplacian = laplace(padded.astype(jnp.float32))
        updated = (
            2.0 * current.astype(jnp.float32) - earlier.astype(jnp.float32) + wave_model * laplacian
        )
        updated = inject_one(updated, source_cell, wavelet[:, moment : moment + 1], anchor).astype(
            jnp.bfloat16
        )
        images.append(laplacian.astype(jnp.bfloat16))
        residuals.append(record_rows(updated, receiver_cell, anchor) - observed[:, moment])
        earlier, current = (current, updated)
    images = list(lax.optimization_barrier(tuple(images)))
    nearer = adjoint_end[0]
    farther = adjoint_end[1]
    gradient = jnp.zeros(velocity.shape, jnp.float32)
    for moment in reversed(range(STEPS)):
        padded = padded_2(nearer, ((DEPTH, 1),), 4)
        laplacian = laplace(padded.astype(jnp.float32))
        updated = (
            2.0 * nearer.astype(jnp.float32) - farther.astype(jnp.float32) + wave_model * laplacian
        )
        updated = inject_rows(updated, receiver_cell, residuals[moment], anchor).astype(jnp.bfloat16)
        gradient = gradient + jnp.sum(
            updated.astype(jnp.float32) * images[moment].astype(jnp.float32), axis=0
        )
        farther, nearer = (nearer, updated)
    step_scale = step_base / math.sqrt(forward_start.shape[1] * lax.axis_size(SHOT))
    summed = reduce_shots(gradient)
    velocity_new = jnp.clip(velocity - step_scale * summed, low_speed, high_speed)
    forward_end = jnp.stack([earlier, current])
    adjoint_start = jnp.stack([nearer, farther])
    return (forward_end, adjoint_start, velocity_new)


def solution(mesh):
    fine = Mesh(mesh.devices.reshape(4, 4, 2, 4, 2), ("y", "zhi", "core", "x", "zlo"))
    placed = (
        P(None, SHOT, DEPTH, None, None),
        P(None, SHOT, DEPTH, None, None),
        P(DEPTH, None, None),
        P(SHOT),
        P(SHOT, None),
        P(SHOT, None),
        P(SHOT, None, None),
    )
    return jax.shard_map(
        body,
        mesh=fine,
        in_specs=placed,
        out_specs=(
            P(None, SHOT, DEPTH, None, None),
            P(None, SHOT, DEPTH, None, None),
            P(DEPTH, None, None),
        ),
        check_vma=False,
    )
```

```python
import math

import jax
import jax.numpy as jnp
from jax import lax
from jax.sharding import Mesh
from jax.sharding import PartitionSpec as P

SHOT = ("y", "zhi", "core")
DEPTH = ("x", "zlo")
CZ = 16
NX = 128
NY = 128
STEPS = 4


stencil_weights = (1.6, -0.2, 8.0 / 315.0, -1.0 / 560.0)
center_weight = -205.0 / 72.0
courant = 0.095
step_base = 0.01
low_speed = 1.5
high_speed = 4.5


def padded_2(cells, sides, width):
    for axis, dim in sides:
        count = lax.axis_size(axis)
        ends = count - 1
        head = lax.slice_in_dim(cells, 0, width, axis=dim)
        tail = lax.slice_in_dim(cells, cells.shape[dim] - width, cells.shape[dim], axis=dim)
        cells = jnp.concatenate(
            [
                lax.ppermute(tail, axis, [(i, (i + 1) % count) for i in range(ends)]),
                cells,
                lax.ppermute(head, axis, [((i + 1) % count, i) for i in range(ends)]),
            ],
            axis=dim,
        )
    return cells


def laplace(depth_padded):
    padded = jnp.pad(depth_padded, ((0, 0), (0, 0), (4, 4), (4, 4)))
    depth_len = padded.shape[1] - 8
    row_len = padded.shape[2] - 8
    column_len = padded.shape[3] - 8

    def window(along_z, along_x, along_y):
        return padded[
            :,
            4 + along_z : 4 + along_z + depth_len,
            4 + along_x : 4 + along_x + row_len,
            4 + along_y : 4 + along_y + column_len,
        ]

    summed = 3.0 * center_weight * window(0, 0, 0)
    for offset in range(1, 5):
        weight = stencil_weights[offset - 1]
        summed = summed + weight * (
            window(offset, 0, 0)
            + window(-offset, 0, 0)
            + window(0, offset, 0)
            + window(0, -offset, 0)
            + window(0, 0, offset)
            + window(0, 0, -offset)
        )
    return summed


def inject(wavefield, cell_ids, values, anchor):
    shot_count = wavefield.shape[0]
    depth_len = wavefield.shape[1]
    plane_size = NX * NY
    planes = cell_ids // plane_size - anchor
    owned_mask = (planes >= 0) & (planes < depth_len)
    flat_index = jnp.clip(planes, 0, depth_len - 1) * plane_size + cell_ids % plane_size
    rows_index = jnp.broadcast_to(jnp.arange(shot_count, dtype=jnp.int32)[:, None], cell_ids.shape)
    flattened = (
        wavefield.reshape(shot_count, -1)
        .at[rows_index, flat_index]
        .add(jnp.where(owned_mask, values, 0.0))
    )
    return flattened.reshape(wavefield.shape)


def cell_coords(cell_ids, anchor):
    plane_size = NX * NY
    planes = cell_ids // plane_size - anchor
    rest = cell_ids % plane_size
    return planes, rest // NY, rest % NY


def inject_one(wavefield, cell_ids, values, anchor):
    planes, rows, columns = cell_coords(cell_ids, anchor)
    shape = wavefield.shape
    hit = (
        (lax.broadcasted_iota(jnp.int32, shape, 1) == planes[:, None, None, None])
        & (lax.broadcasted_iota(jnp.int32, shape, 2) == rows[:, None, None, None])
        & (lax.broadcasted_iota(jnp.int32, shape, 3) == columns[:, None, None, None])
    )
    return jnp.where(hit, wavefield + values[:, :, None, None], wavefield)


def record_rows(wavefield, cell_ids, anchor):
    depth_len = wavefield.shape[1]
    planes, rows, columns = cell_coords(cell_ids, anchor)
    row_ids = jnp.clip(planes, 0, depth_len - 1) * NX + rows
    table = wavefield.reshape(-1, NY)
    choose = row_ids[0][:, None] == lax.broadcasted_iota(jnp.int32, (1, table.shape[0]), 1)
    picked = jnp.dot(choose.astype(table.dtype), table, preferred_element_type=jnp.float32)
    lanes = lax.broadcasted_iota(jnp.int32, picked.shape, 1)
    return jnp.sum(jnp.where(lanes == columns[0][:, None], picked, 0.0), axis=1)[None]


def inject_rows(wavefield, cell_ids, values, anchor):
    depth_len = wavefield.shape[1]
    planes, rows, columns = cell_coords(cell_ids, anchor)
    owned = (planes >= 0) & (planes < depth_len)
    row_ids = jnp.clip(planes, 0, depth_len - 1) * NX + rows
    count = depth_len * NX
    choose = row_ids[0][:, None] == lax.broadcasted_iota(jnp.int32, (1, count), 1)
    lanes = lax.broadcasted_iota(jnp.int32, (cell_ids.shape[1], NY), 1)
    spread = jnp.where(
        (lanes == columns[0][:, None]) & owned[0][:, None], values[0][:, None], 0.0
    )
    high = lax.reduce_precision(spread, exponent_bits=8, mantissa_bits=7)
    rest = spread - high
    middle = lax.reduce_precision(rest, exponent_bits=8, mantissa_bits=7)
    low = rest - middle
    pieces = jnp.concatenate([high, middle, low], axis=1).astype(jnp.bfloat16)
    parts = lax.dot_general(
        choose.astype(jnp.bfloat16),
        pieces,
        (((0,), (0,)), ((), ())),
        preferred_element_type=jnp.float32,
    )
    added = (parts[:, :NY] + parts[:, NY : 2 * NY]) + parts[:, 2 * NY :]
    return wavefield + added.reshape(wavefield.shape)


def record(wavefield, cell_ids, anchor):
    shot_count = wavefield.shape[0]
    plane_size = NX * NY
    planes = cell_ids // plane_size - anchor
    flat_index = jnp.clip(planes, 0, wavefield.shape[1] - 1) * plane_size + cell_ids % plane_size
    return jnp.take_along_axis(wavefield.reshape(shot_count, -1), flat_index, axis=1).astype(
        jnp.float32
    )


def reduce_shots(gradient):
    rows = gradient.reshape(-1, gradient.shape[-1])
    pair = [(0, 1), (1, 0)]
    bit = lax.axis_index("core")
    half = rows.shape[0] // 2
    keep = lax.dynamic_slice_in_dim(rows, bit * half, half, 0)
    send = lax.dynamic_slice_in_dim(rows, (1 - bit) * half, half, 0)
    rows = keep + lax.ppermute(send, "core", pair)
    for axis in ("y", "zhi"):
        count = lax.axis_size(axis)
        me = lax.axis_index(axis)
        part = rows.shape[0] // count
        kept = lax.dynamic_slice_in_dim(rows, me * part, part, 0)
        for shift in range(1, count):
            send = lax.dynamic_slice_in_dim(rows, ((me + shift) % count) * part, part, 0)
            kept = kept + lax.ppermute(send, axis, [(i, (i + shift) % count) for i in range(count)])
        rows = kept
    for axis in ("zhi", "y"):
        count = lax.axis_size(axis)
        me = lax.axis_index(axis)
        part = rows.shape[0]
        whole = jnp.zeros((count * part, rows.shape[1]), rows.dtype)
        whole = lax.dynamic_update_slice_in_dim(whole, rows, me * part, 0)
        for shift in range(1, count):
            got = lax.ppermute(rows, axis, [(i, (i + shift) % count) for i in range(count)])
            whole = lax.dynamic_update_slice_in_dim(whole, got, ((me - shift) % count) * part, 0)
        rows = whole
    other = lax.ppermute(rows, "core", pair)
    rows = jnp.where(bit == 0, jnp.concatenate([rows, other]), jnp.concatenate([other, rows]))
    return rows.reshape(gradient.shape)


def body(forward_start, adjoint_end, velocity, source_cell, wavelet, receiver_cell, observed):
    anchor = lax.axis_index(DEPTH) * CZ
    wave_model = (courant * velocity) ** 2
    source_ids = source_cell[:, None]
    images = []
    residuals = []
    earlier = forward_start[0]
    current = forward_start[1]
    both = padded_2(jnp.concatenate([current, adjoint_end[0]]), ((DEPTH, 1),), 4)
    first_padded, adjoint_padded = both[:1], both[1:]
    for moment in range(STEPS):
        padded = first_padded if moment == 0 else padded_2(current, ((DEPTH, 1),), 4)
        laplacian = laplace(padded.astype(jnp.float32))
        updated = (
            2.0 * current.astype(jnp.float32) - earlier.astype(jnp.float32) + wave_model * laplacian
        )
        updated = inject_one(updated, source_cell, wavelet[:, moment : moment + 1], anchor).astype(
            jnp.bfloat16
        )
        images.append(laplacian.astype(jnp.bfloat16))
        residuals.append(record_rows(updated, receiver_cell, anchor) - observed[:, moment])
        earlier, current = (current, updated)
    images = list(lax.optimization_barrier(tuple(images)))
    nearer = adjoint_end[0]
    farther = adjoint_end[1]
    gradient = jnp.zeros(velocity.shape, jnp.float32)
    for moment in reversed(range(STEPS)):
        padded = adjoint_padded if moment == STEPS - 1 else padded_2(nearer, ((DEPTH, 1),), 4)
        laplacian = laplace(padded.astype(jnp.float32))
        updated = (
            2.0 * nearer.astype(jnp.float32) - farther.astype(jnp.float32) + wave_model * laplacian
        )
        updated = inject_rows(updated, receiver_cell, residuals[moment], anchor).astype(jnp.bfloat16)
        gradient = gradient + jnp.sum(
            updated.astype(jnp.float32) * images[moment].astype(jnp.float32), axis=0
        )
        farther, nearer = (nearer, updated)
    step_scale = step_base / math.sqrt(forward_start.shape[1] * lax.axis_size(SHOT))
    summed = reduce_shots(gradient)
    velocity_new = jnp.clip(velocity - step_scale * summed, low_speed, high_speed)
    forward_end = jnp.stack([earlier, current])
    adjoint_start = jnp.stack([nearer, farther])
    return (forward_end, adjoint_start, velocity_new)


def solution(mesh):
    fine = Mesh(mesh.devices.reshape(4, 4, 2, 4, 2), ("y", "zhi", "core", "x", "zlo"))
    placed = (
        P(None, SHOT, DEPTH, None, None),
        P(None, SHOT, DEPTH, None, None),
        P(DEPTH, None, None),
        P(SHOT),
        P(SHOT, None),
        P(SHOT, None),
        P(SHOT, None, None),
    )
    return jax.shard_map(
        body,
        mesh=fine,
        in_specs=placed,
        out_specs=(
            P(None, SHOT, DEPTH, None, None),
            P(None, SHOT, DEPTH, None, None),
            P(DEPTH, None, None),
        ),
        check_vma=False,
    )
```

```python
import math

import jax
import jax.numpy as jnp
from jax import lax
from jax.sharding import Mesh
from jax.sharding import PartitionSpec as P

SHOT = ("y", "zhi", "core")
DEPTH = ("x", "zlo")
CZ = 16
NX = 128
NY = 128
STEPS = 4


stencil_weights = (1.6, -0.2, 8.0 / 315.0, -1.0 / 560.0)
center_weight = -205.0 / 72.0
courant = 0.095
step_base = 0.01
low_speed = 1.5
high_speed = 4.5


def padded_2(cells, sides, width):
    for axis, dim in sides:
        count = lax.axis_size(axis)
        ends = count - 1
        head = lax.slice_in_dim(cells, 0, width, axis=dim)
        tail = lax.slice_in_dim(cells, cells.shape[dim] - width, cells.shape[dim], axis=dim)
        cells = jnp.concatenate(
            [
                lax.ppermute(tail, axis, [(i, (i + 1) % count) for i in range(ends)]),
                cells,
                lax.ppermute(head, axis, [((i + 1) % count, i) for i in range(ends)]),
            ],
            axis=dim,
        )
    return cells


def laplace(depth_padded):
    padded = jnp.pad(depth_padded, ((0, 0), (0, 0), (4, 4), (4, 4)))
    depth_len = padded.shape[1] - 8
    row_len = padded.shape[2] - 8
    column_len = padded.shape[3] - 8

    def window(along_z, along_x, along_y):
        return padded[
            :,
            4 + along_z : 4 + along_z + depth_len,
            4 + along_x : 4 + along_x + row_len,
            4 + along_y : 4 + along_y + column_len,
        ]

    summed = 3.0 * center_weight * window(0, 0, 0)
    for offset in range(1, 5):
        weight = stencil_weights[offset - 1]
        summed = summed + weight * (
            window(offset, 0, 0)
            + window(-offset, 0, 0)
            + window(0, offset, 0)
            + window(0, -offset, 0)
            + window(0, 0, offset)
            + window(0, 0, -offset)
        )
    return summed


def inject(wavefield, cell_ids, values, anchor):
    shot_count = wavefield.shape[0]
    depth_len = wavefield.shape[1]
    plane_size = NX * NY
    planes = cell_ids // plane_size - anchor
    owned_mask = (planes >= 0) & (planes < depth_len)
    flat_index = jnp.clip(planes, 0, depth_len - 1) * plane_size + cell_ids % plane_size
    rows_index = jnp.broadcast_to(jnp.arange(shot_count, dtype=jnp.int32)[:, None], cell_ids.shape)
    flattened = (
        wavefield.reshape(shot_count, -1)
        .at[rows_index, flat_index]
        .add(jnp.where(owned_mask, values, 0.0))
    )
    return flattened.reshape(wavefield.shape)


def cell_coords(cell_ids, anchor):
    plane_size = NX * NY
    planes = cell_ids // plane_size - anchor
    rest = cell_ids % plane_size
    return planes, rest // NY, rest % NY


def inject_one(wavefield, cell_ids, values, anchor):
    planes, rows, columns = cell_coords(cell_ids, anchor)
    shape = wavefield.shape
    hit = (
        (lax.broadcasted_iota(jnp.int32, shape, 1) == planes[:, None, None, None])
        & (lax.broadcasted_iota(jnp.int32, shape, 2) == rows[:, None, None, None])
        & (lax.broadcasted_iota(jnp.int32, shape, 3) == columns[:, None, None, None])
    )
    return jnp.where(hit, wavefield + values[:, :, None, None], wavefield)


def record_rows(wavefield, cell_ids, anchor):
    depth_len = wavefield.shape[1]
    planes, rows, columns = cell_coords(cell_ids, anchor)
    row_ids = jnp.clip(planes, 0, depth_len - 1) * NX + rows
    table = wavefield.reshape(-1, NY)
    choose = row_ids[0][:, None] == lax.broadcasted_iota(jnp.int32, (1, table.shape[0]), 1)
    picked = jnp.dot(choose.astype(table.dtype), table, preferred_element_type=jnp.float32)
    lanes = lax.broadcasted_iota(jnp.int32, picked.shape, 1)
    return jnp.sum(jnp.where(lanes == columns[0][:, None], picked, 0.0), axis=1)[None]


def receiver_terms(cell_ids, values, anchor, depth_len):
    planes, rows, columns = cell_coords(cell_ids, anchor)
    owned = (planes >= 0) & (planes < depth_len)
    row_ids = jnp.clip(planes, 0, depth_len - 1) * NX + rows
    count = depth_len * NX
    choose = row_ids[0][:, None] == lax.broadcasted_iota(jnp.int32, (1, count), 1)
    lanes = lax.broadcasted_iota(jnp.int32, (cell_ids.shape[1], NY), 1)
    spread = jnp.where(
        (lanes == columns[0][:, None]) & owned[0][:, None], values[0][:, None], 0.0
    )
    high = lax.reduce_precision(spread, exponent_bits=8, mantissa_bits=7)
    rest = spread - high
    middle = lax.reduce_precision(rest, exponent_bits=8, mantissa_bits=7)
    low = rest - middle
    pieces = jnp.concatenate([high, middle, low], axis=1).astype(jnp.bfloat16)
    parts = lax.dot_general(
        choose.astype(jnp.bfloat16),
        pieces,
        (((0,), (0,)), ((), ())),
        preferred_element_type=jnp.float32,
    )
    added = (parts[:, :NY] + parts[:, NY : 2 * NY]) + parts[:, 2 * NY :]
    return added.reshape(1, depth_len, NX, NY)


def record(wavefield, cell_ids, anchor):
    shot_count = wavefield.shape[0]
    plane_size = NX * NY
    planes = cell_ids // plane_size - anchor
    flat_index = jnp.clip(planes, 0, wavefield.shape[1] - 1) * plane_size + cell_ids % plane_size
    return jnp.take_along_axis(wavefield.reshape(shot_count, -1), flat_index, axis=1).astype(
        jnp.float32
    )


def reduce_shots(gradient):
    rows = gradient.reshape(-1, gradient.shape[-1])
    pair = [(0, 1), (1, 0)]
    bit = lax.axis_index("core")
    half = rows.shape[0] // 2
    keep = lax.dynamic_slice_in_dim(rows, bit * half, half, 0)
    send = lax.dynamic_slice_in_dim(rows, (1 - bit) * half, half, 0)
    rows = keep + lax.ppermute(send, "core", pair)
    for axis in ("y", "zhi"):
        count = lax.axis_size(axis)
        me = lax.axis_index(axis)
        part = rows.shape[0] // count
        kept = lax.dynamic_slice_in_dim(rows, me * part, part, 0)
        for shift in range(1, count):
            send = lax.dynamic_slice_in_dim(rows, ((me + shift) % count) * part, part, 0)
            kept = kept + lax.ppermute(send, axis, [(i, (i + shift) % count) for i in range(count)])
        rows = kept
    for axis in ("zhi", "y"):
        count = lax.axis_size(axis)
        me = lax.axis_index(axis)
        part = rows.shape[0]
        whole = jnp.zeros((count * part, rows.shape[1]), rows.dtype)
        whole = lax.dynamic_update_slice_in_dim(whole, rows, me * part, 0)
        for shift in range(1, count):
            got = lax.ppermute(rows, axis, [(i, (i + shift) % count) for i in range(count)])
            whole = lax.dynamic_update_slice_in_dim(whole, got, ((me - shift) % count) * part, 0)
        rows = whole
    other = lax.ppermute(rows, "core", pair)
    rows = jnp.where(bit == 0, jnp.concatenate([rows, other]), jnp.concatenate([other, rows]))
    return rows.reshape(gradient.shape)


def edges(cells, width):
    count = lax.axis_size(DEPTH)
    below = lax.ppermute(cells[:, -width:], DEPTH, [(i, i + 1) for i in range(count - 1)])
    above = lax.ppermute(cells[:, :width], DEPTH, [(i + 1, i) for i in range(count - 1)])
    return below, above


def around(cells, below, above, width):
    depth = below.shape[1]
    return jnp.concatenate(
        [below[:, depth - width :], cells, above[:, :width]], axis=1
    )


def leap(current, earlier, model, stencil, extra):
    updated = 2.0 * current.astype(jnp.float32) - earlier.astype(jnp.float32) + model * stencil
    return updated + extra


def body(forward_start, adjoint_end, velocity, source_cell, wavelet, receiver_cell, observed):
    depth_len = velocity.shape[0]
    anchor = lax.axis_index(DEPTH) * depth_len
    wide = anchor - 4
    wave_model = ((courant * velocity) ** 2)[None]
    model_below, model_above = edges(wave_model, 4)
    model_wide = around(wave_model, model_below, model_above, 4)
    zeros_own = jnp.zeros(forward_start.shape[1:], jnp.float32)
    zeros_wide = jnp.zeros(model_wide.shape, jnp.float32)

    def source(moment, zeros, base):
        return inject_one(zeros, source_cell, wavelet[:, moment : moment + 1], base)

    first, second = forward_start[0], forward_start[1]
    nearer, farther = adjoint_end[0], adjoint_end[1]
    pair_below, pair_above = edges(
        jnp.concatenate(
            [first[:, :4], second[:, :8], nearer[:, :4], first[:, -4:], second[:, -8:], nearer[:, -4:]],
            axis=1,
        ),
        16,
    )
    images = []
    residuals = []
    second_pad, first_wide, model_wide = lax.optimization_barrier((
        jnp.concatenate([pair_below[:, 4:12], second, pair_above[:, 4:12]], axis=1),
        jnp.concatenate([pair_below[:, 0:4], first, pair_above[:, 0:4]], axis=1),
        model_wide,
    ))
    stencil = laplace(second_pad.astype(jnp.float32))
    wide_next = leap(second_pad[:, 4:-4], first_wide, model_wide, stencil, source(0, zeros_wide, wide)).astype(jnp.bfloat16)
    wide_next = lax.optimization_barrier(wide_next)
    images.append(stencil[:, 4:-4].astype(jnp.bfloat16))
    residuals.append(record_rows(wide_next, receiver_cell, wide) - observed[:, 0])
    stencil = laplace(wide_next.astype(jnp.float32))
    own_next = leap(wide_next[:, 4:-4], second, wave_model, stencil, source(1, zeros_own, anchor)).astype(jnp.bfloat16)
    images.append(stencil.astype(jnp.bfloat16))
    residuals.append(record_rows(own_next, receiver_cell, anchor) - observed[:, 1])
    below, above = edges(own_next, 8)
    third_pad = lax.optimization_barrier(around(own_next, below, above, 8))
    stencil = laplace(third_pad.astype(jnp.float32))
    wide_four = leap(third_pad[:, 4:-4], wide_next, model_wide, stencil, source(2, zeros_wide, wide)).astype(jnp.bfloat16)
    wide_four = lax.optimization_barrier(wide_four)
    images.append(stencil[:, 4:-4].astype(jnp.bfloat16))
    residuals.append(record_rows(wide_four, receiver_cell, wide) - observed[:, 2])
    stencil = laplace(wide_four.astype(jnp.float32))
    own_five = leap(wide_four[:, 4:-4], own_next, wave_model, stencil, source(3, zeros_own, anchor)).astype(jnp.bfloat16)
    images.append(stencil.astype(jnp.bfloat16))
    residuals.append(record_rows(own_five, receiver_cell, anchor) - observed[:, 3])
    forward_end = jnp.stack([wide_four[:, 4:-4], own_five])
    images = list(lax.optimization_barrier(tuple(images)))

    injected = [
        receiver_terms(receiver_cell, residuals[0], anchor, depth_len),
        receiver_terms(receiver_cell, residuals[1], anchor, depth_len),
        receiver_terms(receiver_cell, residuals[2], wide, depth_len + 8),
        receiver_terms(receiver_cell, residuals[3], anchor, depth_len),
    ]
    five_pad = lax.optimization_barrier(
        jnp.concatenate([pair_below[:, 12:16], nearer, pair_above[:, 12:16]], axis=1)
    )
    stencil = laplace(five_pad.astype(jnp.float32))
    q4 = leap(nearer, farther, wave_model, stencil, injected[3]).astype(jnp.bfloat16)
    below, above = edges(q4, 8)
    four_pad = lax.optimization_barrier(around(q4, below, above, 8))
    stencil = laplace(four_pad.astype(jnp.float32))
    q3_wide = leap(four_pad[:, 4:-4], five_pad, model_wide, stencil, injected[2]).astype(jnp.bfloat16)
    q3_wide = lax.optimization_barrier(q3_wide)
    stencil = laplace(q3_wide.astype(jnp.float32))
    q2 = leap(q3_wide[:, 4:-4], q4, wave_model, stencil, injected[1]).astype(jnp.bfloat16)
    below, above = edges(q2, 4)
    two_pad = around(q2, below, above, 4)
    stencil = laplace(two_pad.astype(jnp.float32))
    q1 = leap(q2, q3_wide[:, 4:-4], wave_model, stencil, injected[0]).astype(jnp.bfloat16)

    gradient = jnp.zeros(velocity.shape, jnp.float32)
    for field, image in ((q4, images[3]), (q3_wide[:, 4:-4], images[2]), (q2, images[1]), (q1, images[0])):
        gradient = gradient + jnp.sum(field.astype(jnp.float32) * image.astype(jnp.float32), axis=0)
    step_scale = step_base / math.sqrt(forward_start.shape[1] * lax.axis_size(SHOT))
    summed = reduce_shots(gradient)
    velocity_new = jnp.clip(velocity - step_scale * summed, low_speed, high_speed)
    adjoint_start = jnp.stack([q1, q2])
    return (forward_end, adjoint_start, velocity_new)


def solution(mesh):
    fine = Mesh(mesh.devices.reshape(4, 4, 2, 4, 2), ("y", "zhi", "core", "x", "zlo"))
    placed = (
        P(None, SHOT, DEPTH, None, None),
        P(None, SHOT, DEPTH, None, None),
        P(DEPTH, None, None),
        P(SHOT),
        P(SHOT, None),
        P(SHOT, None),
        P(SHOT, None, None),
    )
    return jax.shard_map(
        body,
        mesh=fine,
        in_specs=placed,
        out_specs=(
            P(None, SHOT, DEPTH, None, None),
            P(None, SHOT, DEPTH, None, None),
            P(DEPTH, None, None),
        ),
        check_vma=False,
    )
```

```python
import math

import jax
import jax.numpy as jnp
from jax import lax
from jax.sharding import Mesh
from jax.sharding import PartitionSpec as P

SHOT = ("y", "zhi", "core")
DEPTH = ("x", "zlo")
CZ = 16
NX = 128
NY = 128
STEPS = 4


stencil_weights = (1.6, -0.2, 8.0 / 315.0, -1.0 / 560.0)
center_weight = -205.0 / 72.0
courant = 0.095
step_base = 0.01
low_speed = 1.5
high_speed = 4.5


def padded_2(cells, sides, width):
    for axis, dim in sides:
        count = lax.axis_size(axis)
        ends = count - 1
        head = lax.slice_in_dim(cells, 0, width, axis=dim)
        tail = lax.slice_in_dim(cells, cells.shape[dim] - width, cells.shape[dim], axis=dim)
        cells = jnp.concatenate(
            [
                lax.ppermute(tail, axis, [(i, (i + 1) % count) for i in range(ends)]),
                cells,
                lax.ppermute(head, axis, [((i + 1) % count, i) for i in range(ends)]),
            ],
            axis=dim,
        )
    return cells


def laplace(depth_padded):
    padded = jnp.pad(depth_padded, ((0, 0), (0, 0), (4, 4), (4, 4)))
    depth_len = padded.shape[1] - 8
    row_len = padded.shape[2] - 8
    column_len = padded.shape[3] - 8

    def window(along_z, along_x, along_y):
        return padded[
            :,
            4 + along_z : 4 + along_z + depth_len,
            4 + along_x : 4 + along_x + row_len,
            4 + along_y : 4 + along_y + column_len,
        ]

    summed = 3.0 * center_weight * window(0, 0, 0)
    for offset in range(1, 5):
        weight = stencil_weights[offset - 1]
        summed = summed + weight * (
            window(offset, 0, 0)
            + window(-offset, 0, 0)
            + window(0, offset, 0)
            + window(0, -offset, 0)
            + window(0, 0, offset)
            + window(0, 0, -offset)
        )
    return summed


def inject(wavefield, cell_ids, values, anchor):
    shot_count = wavefield.shape[0]
    depth_len = wavefield.shape[1]
    plane_size = NX * NY
    planes = cell_ids // plane_size - anchor
    owned_mask = (planes >= 0) & (planes < depth_len)
    flat_index = jnp.clip(planes, 0, depth_len - 1) * plane_size + cell_ids % plane_size
    rows_index = jnp.broadcast_to(jnp.arange(shot_count, dtype=jnp.int32)[:, None], cell_ids.shape)
    flattened = (
        wavefield.reshape(shot_count, -1)
        .at[rows_index, flat_index]
        .add(jnp.where(owned_mask, values, 0.0))
    )
    return flattened.reshape(wavefield.shape)


def cell_coords(cell_ids, anchor):
    plane_size = NX * NY
    planes = cell_ids // plane_size - anchor
    rest = cell_ids % plane_size
    return planes, rest // NY, rest % NY


def inject_one(wavefield, cell_ids, values, anchor):
    planes, rows, columns = cell_coords(cell_ids, anchor)
    shape = wavefield.shape
    hit = (
        (lax.broadcasted_iota(jnp.int32, shape, 1) == planes[:, None, None, None])
        & (lax.broadcasted_iota(jnp.int32, shape, 2) == rows[:, None, None, None])
        & (lax.broadcasted_iota(jnp.int32, shape, 3) == columns[:, None, None, None])
    )
    return jnp.where(hit, wavefield + values[:, :, None, None], wavefield)


def record_rows(wavefield, cell_ids, anchor):
    depth_len = wavefield.shape[1]
    planes, rows, columns = cell_coords(cell_ids, anchor)
    row_ids = jnp.clip(planes, 0, depth_len - 1) * NX + rows
    table = wavefield.reshape(-1, NY)
    choose = row_ids[0][:, None] == lax.broadcasted_iota(jnp.int32, (1, table.shape[0]), 1)
    picked = jnp.dot(choose.astype(table.dtype), table, preferred_element_type=jnp.float32)
    lanes = lax.broadcasted_iota(jnp.int32, picked.shape, 1)
    return jnp.sum(jnp.where(lanes == columns[0][:, None], picked, 0.0), axis=1)[None]


def inject_rows(wavefield, cell_ids, values, anchor):
    depth_len = wavefield.shape[1]
    planes, rows, columns = cell_coords(cell_ids, anchor)
    owned = (planes >= 0) & (planes < depth_len)
    row_ids = jnp.clip(planes, 0, depth_len - 1) * NX + rows
    count = depth_len * NX
    choose = row_ids[0][:, None] == lax.broadcasted_iota(jnp.int32, (1, count), 1)
    lanes = lax.broadcasted_iota(jnp.int32, (cell_ids.shape[1], NY), 1)
    spread = jnp.where(
        (lanes == columns[0][:, None]) & owned[0][:, None], values[0][:, None], 0.0
    )
    high = lax.reduce_precision(spread, exponent_bits=8, mantissa_bits=7)
    rest = spread - high
    middle = lax.reduce_precision(rest, exponent_bits=8, mantissa_bits=7)
    low = rest - middle
    pieces = jnp.concatenate([high, middle, low], axis=1).astype(jnp.bfloat16)
    parts = lax.dot_general(
        choose.astype(jnp.bfloat16),
        pieces,
        (((0,), (0,)), ((), ())),
        preferred_element_type=jnp.float32,
    )
    added = (parts[:, :NY] + parts[:, NY : 2 * NY]) + parts[:, 2 * NY :]
    return wavefield + added.reshape(wavefield.shape)


def record(wavefield, cell_ids, anchor):
    shot_count = wavefield.shape[0]
    plane_size = NX * NY
    planes = cell_ids // plane_size - anchor
    flat_index = jnp.clip(planes, 0, wavefield.shape[1] - 1) * plane_size + cell_ids % plane_size
    return jnp.take_along_axis(wavefield.reshape(shot_count, -1), flat_index, axis=1).astype(
        jnp.float32
    )


def reduce_shots(gradient, finish):
    rows = gradient.reshape(-1, gradient.shape[-1])
    pair = [(0, 1), (1, 0)]
    bit = lax.axis_index("core")
    half = rows.shape[0] // 2
    keep = lax.dynamic_slice_in_dim(rows, bit * half, half, 0)
    send = lax.dynamic_slice_in_dim(rows, (1 - bit) * half, half, 0)
    rows = keep + lax.ppermute(send, "core", pair)
    offset = bit * half
    for axis in ("y", "zhi"):
        count = lax.axis_size(axis)
        me = lax.axis_index(axis)
        part = rows.shape[0] // count
        kept = lax.dynamic_slice_in_dim(rows, me * part, part, 0)
        for shift in range(1, count):
            send = lax.dynamic_slice_in_dim(rows, ((me + shift) % count) * part, part, 0)
            kept = kept + lax.ppermute(send, axis, [(i, (i + shift) % count) for i in range(count)])
        rows = kept
        offset = offset + me * part
    rows = finish(rows, offset)
    for axis in ("zhi", "y"):
        count = lax.axis_size(axis)
        me = lax.axis_index(axis)
        part = rows.shape[0]
        whole = jnp.zeros((count * part, rows.shape[1]), rows.dtype)
        whole = lax.dynamic_update_slice_in_dim(whole, rows, me * part, 0)
        for shift in range(1, count):
            got = lax.ppermute(rows, axis, [(i, (i + shift) % count) for i in range(count)])
            whole = lax.dynamic_update_slice_in_dim(whole, got, ((me - shift) % count) * part, 0)
        rows = whole
    other = lax.ppermute(rows, "core", pair)
    rows = jnp.where(bit == 0, jnp.concatenate([rows, other]), jnp.concatenate([other, rows]))
    return rows.reshape(gradient.shape)


def body(forward_start, adjoint_end, velocity, source_cell, wavelet, receiver_cell, observed):
    anchor = lax.axis_index(DEPTH) * CZ
    wave_model = (courant * velocity) ** 2
    source_ids = source_cell[:, None]
    images = []
    residuals = []
    earlier = forward_start[0]
    current = forward_start[1]
    both = padded_2(jnp.concatenate([current, adjoint_end[0]]), ((DEPTH, 1),), 4)
    first_padded, adjoint_padded = both[:1], both[1:]
    for moment in range(STEPS):
        padded = first_padded if moment == 0 else padded_2(current, ((DEPTH, 1),), 4)
        laplacian = laplace(padded.astype(jnp.float32))
        updated = (
            2.0 * current.astype(jnp.float32) - earlier.astype(jnp.float32) + wave_model * laplacian
        )
        updated = inject_one(updated, source_cell, wavelet[:, moment : moment + 1], anchor).astype(
            jnp.bfloat16
        )
        images.append(laplacian.astype(jnp.bfloat16))
        residuals.append(record_rows(updated, receiver_cell, anchor) - observed[:, moment])
        earlier, current = (current, updated)
    images = list(lax.optimization_barrier(tuple(images)))
    nearer = adjoint_end[0]
    farther = adjoint_end[1]
    gradient = jnp.zeros(velocity.shape, jnp.float32)
    for moment in reversed(range(STEPS)):
        padded = adjoint_padded if moment == STEPS - 1 else padded_2(nearer, ((DEPTH, 1),), 4)
        laplacian = laplace(padded.astype(jnp.float32))
        updated = (
            2.0 * nearer.astype(jnp.float32) - farther.astype(jnp.float32) + wave_model * laplacian
        )
        updated = inject_rows(updated, receiver_cell, residuals[moment], anchor).astype(jnp.bfloat16)
        gradient = gradient + jnp.sum(
            updated.astype(jnp.float32) * images[moment].astype(jnp.float32), axis=0
        )
        farther, nearer = (nearer, updated)
    step_scale = step_base / math.sqrt(forward_start.shape[1] * lax.axis_size(SHOT))
    speed_rows = velocity.reshape(-1, velocity.shape[-1])

    def finish(summed, offset):
        speed = lax.dynamic_slice_in_dim(speed_rows, offset, summed.shape[0], 0)
        return jnp.clip(speed - step_scale * summed, low_speed, high_speed)

    velocity_new = reduce_shots(gradient, finish)
    forward_end = jnp.stack([earlier, current])
    adjoint_start = jnp.stack([nearer, farther])
    return (forward_end, adjoint_start, velocity_new)


def solution(mesh):
    fine = Mesh(mesh.devices.reshape(4, 4, 2, 4, 2), ("y", "zhi", "core", "x", "zlo"))
    placed = (
        P(None, SHOT, DEPTH, None, None),
        P(None, SHOT, DEPTH, None, None),
        P(DEPTH, None, None),
        P(SHOT),
        P(SHOT, None),
        P(SHOT, None),
        P(SHOT, None, None),
    )
    return jax.shard_map(
        body,
        mesh=fine,
        in_specs=placed,
        out_specs=(
            P(None, SHOT, DEPTH, None, None),
            P(None, SHOT, DEPTH, None, None),
            P(DEPTH, None, None),
        ),
        check_vma=False,
    )
```

```python
import math

import jax
import jax.numpy as jnp
from jax import lax
from jax.sharding import Mesh
from jax.sharding import PartitionSpec as P

SHOT = ("y", "zhi", "core")
DEPTH = ("x", "zlo")
CZ = 16
NX = 128
NY = 128
STEPS = 4


stencil_weights = (1.6, -0.2, 8.0 / 315.0, -1.0 / 560.0)
center_weight = -205.0 / 72.0
courant = 0.095
step_base = 0.01
low_speed = 1.5
high_speed = 4.5


def padded_2(cells, sides, width):
    for axis, dim in sides:
        count = lax.axis_size(axis)
        ends = count - 1
        head = lax.slice_in_dim(cells, 0, width, axis=dim)
        tail = lax.slice_in_dim(cells, cells.shape[dim] - width, cells.shape[dim], axis=dim)
        cells = jnp.concatenate(
            [
                lax.ppermute(tail, axis, [(i, (i + 1) % count) for i in range(ends)]),
                cells,
                lax.ppermute(head, axis, [((i + 1) % count, i) for i in range(ends)]),
            ],
            axis=dim,
        )
    return cells


def laplace(depth_padded):
    padded = jnp.pad(depth_padded, ((0, 0), (0, 0), (4, 4), (4, 4)))
    depth_len = padded.shape[1] - 8
    row_len = padded.shape[2] - 8
    column_len = padded.shape[3] - 8

    def window(along_z, along_x, along_y):
        return padded[
            :,
            4 + along_z : 4 + along_z + depth_len,
            4 + along_x : 4 + along_x + row_len,
            4 + along_y : 4 + along_y + column_len,
        ]

    summed = 3.0 * center_weight * window(0, 0, 0)
    for offset in range(1, 5):
        weight = stencil_weights[offset - 1]
        summed = summed + weight * (
            window(offset, 0, 0)
            + window(-offset, 0, 0)
            + window(0, offset, 0)
            + window(0, -offset, 0)
            + window(0, 0, offset)
            + window(0, 0, -offset)
        )
    return summed


def inject(wavefield, cell_ids, values, anchor):
    shot_count = wavefield.shape[0]
    depth_len = wavefield.shape[1]
    plane_size = NX * NY
    planes = cell_ids // plane_size - anchor
    owned_mask = (planes >= 0) & (planes < depth_len)
    flat_index = jnp.clip(planes, 0, depth_len - 1) * plane_size + cell_ids % plane_size
    rows_index = jnp.broadcast_to(jnp.arange(shot_count, dtype=jnp.int32)[:, None], cell_ids.shape)
    flattened = (
        wavefield.reshape(shot_count, -1)
        .at[rows_index, flat_index]
        .add(jnp.where(owned_mask, values, 0.0))
    )
    return flattened.reshape(wavefield.shape)


def cell_coords(cell_ids, anchor):
    plane_size = NX * NY
    planes = cell_ids // plane_size - anchor
    rest = cell_ids % plane_size
    return planes, rest // NY, rest % NY


def inject_one(wavefield, cell_ids, values, anchor):
    planes, rows, columns = cell_coords(cell_ids, anchor)
    shape = wavefield.shape
    hit = (
        (lax.broadcasted_iota(jnp.int32, shape, 1) == planes[:, None, None, None])
        & (lax.broadcasted_iota(jnp.int32, shape, 2) == rows[:, None, None, None])
        & (lax.broadcasted_iota(jnp.int32, shape, 3) == columns[:, None, None, None])
    )
    return jnp.where(hit, wavefield + values[:, :, None, None], wavefield)


def record_rows(wavefield, cell_ids, anchor):
    depth_len = wavefield.shape[1]
    planes, rows, columns = cell_coords(cell_ids, anchor)
    row_ids = jnp.clip(planes, 0, depth_len - 1) * NX + rows
    table = wavefield.reshape(-1, NY)
    choose = row_ids[0][:, None] == lax.broadcasted_iota(jnp.int32, (1, table.shape[0]), 1)
    picked = jnp.dot(choose.astype(table.dtype), table, preferred_element_type=jnp.float32)
    lanes = lax.broadcasted_iota(jnp.int32, picked.shape, 1)
    return jnp.sum(jnp.where(lanes == columns[0][:, None], picked, 0.0), axis=1)[None]


def inject_rows(wavefield, cell_ids, values, anchor):
    depth_len = wavefield.shape[1]
    planes, rows, columns = cell_coords(cell_ids, anchor)
    owned = (planes >= 0) & (planes < depth_len)
    row_ids = jnp.clip(planes, 0, depth_len - 1) * NX + rows
    count = depth_len * NX
    choose = row_ids[0][:, None] == lax.broadcasted_iota(jnp.int32, (1, count), 1)
    lanes = lax.broadcasted_iota(jnp.int32, (cell_ids.shape[1], NY), 1)
    spread = jnp.where(
        (lanes == columns[0][:, None]) & owned[0][:, None], values[0][:, None], 0.0
    )
    high = lax.reduce_precision(spread, exponent_bits=8, mantissa_bits=7)
    rest = spread - high
    middle = lax.reduce_precision(rest, exponent_bits=8, mantissa_bits=7)
    low = rest - middle
    pieces = jnp.concatenate([high, middle, low], axis=1).astype(jnp.bfloat16)
    parts = lax.dot_general(
        choose.astype(jnp.bfloat16),
        pieces,
        (((0,), (0,)), ((), ())),
        preferred_element_type=jnp.float32,
    )
    added = (parts[:, :NY] + parts[:, NY : 2 * NY]) + parts[:, 2 * NY :]
    return wavefield + added.reshape(wavefield.shape)


def record(wavefield, cell_ids, anchor):
    shot_count = wavefield.shape[0]
    plane_size = NX * NY
    planes = cell_ids // plane_size - anchor
    flat_index = jnp.clip(planes, 0, wavefield.shape[1] - 1) * plane_size + cell_ids % plane_size
    return jnp.take_along_axis(wavefield.reshape(shot_count, -1), flat_index, axis=1).astype(
        jnp.float32
    )


def reduce_shots(gradient, finish):
    rows = gradient.reshape(-1, gradient.shape[-1])
    pair = [(0, 1), (1, 0)]
    bit = lax.axis_index("core")
    half = rows.shape[0] // 2
    keep = lax.dynamic_slice_in_dim(rows, bit * half, half, 0)
    send = lax.dynamic_slice_in_dim(rows, (1 - bit) * half, half, 0)
    rows = keep + lax.ppermute(send, "core", pair)
    offset = bit * half
    for axis in ("y", "zhi"):
        count = lax.axis_size(axis)
        me = lax.axis_index(axis)
        part = rows.shape[0] // count
        kept = lax.dynamic_slice_in_dim(rows, me * part, part, 0)
        for shift in range(1, count):
            send = lax.dynamic_slice_in_dim(rows, ((me + shift) % count) * part, part, 0)
            kept = kept + lax.ppermute(send, axis, [(i, (i + shift) % count) for i in range(count)])
        rows = kept
        offset = offset + me * part
    rows = finish(rows, offset)
    for axis in ("zhi", "y"):
        count = lax.axis_size(axis)
        me = lax.axis_index(axis)
        part = rows.shape[0]
        whole = jnp.zeros((count * part, rows.shape[1]), rows.dtype)
        whole = lax.dynamic_update_slice_in_dim(whole, rows, me * part, 0)
        for shift in range(1, count):
            got = lax.ppermute(rows, axis, [(i, (i + shift) % count) for i in range(count)])
            whole = lax.dynamic_update_slice_in_dim(whole, got, ((me - shift) % count) * part, 0)
        rows = whole
    other = lax.ppermute(rows, "core", pair)
    whole = jnp.zeros((2 * rows.shape[0], rows.shape[1]), rows.dtype)
    whole = lax.dynamic_update_slice_in_dim(whole, rows, bit * rows.shape[0], 0)
    whole = lax.dynamic_update_slice_in_dim(whole, other, (1 - bit) * rows.shape[0], 0)
    return whole.reshape(gradient.shape)


def body(forward_start, adjoint_end, velocity, source_cell, wavelet, receiver_cell, observed):
    anchor = lax.axis_index(DEPTH) * CZ
    wave_model = (courant * velocity) ** 2
    source_ids = source_cell[:, None]
    images = []
    residuals = []
    earlier = forward_start[0]
    current = forward_start[1]
    both = padded_2(jnp.concatenate([current, adjoint_end[0]]), ((DEPTH, 1),), 4)
    first_padded, adjoint_padded = both[:1], both[1:]
    for moment in range(STEPS):
        padded = first_padded if moment == 0 else padded_2(current, ((DEPTH, 1),), 4)
        laplacian = laplace(padded.astype(jnp.float32))
        updated = (
            2.0 * current.astype(jnp.float32) - earlier.astype(jnp.float32) + wave_model * laplacian
        )
        updated = inject_one(updated, source_cell, wavelet[:, moment : moment + 1], anchor).astype(
            jnp.bfloat16
        )
        images.append(laplacian.astype(jnp.bfloat16))
        residuals.append(record_rows(updated, receiver_cell, anchor) - observed[:, moment])
        earlier, current = (current, updated)
    images = list(lax.optimization_barrier(tuple(images)))
    nearer = adjoint_end[0]
    farther = adjoint_end[1]
    gradient = jnp.zeros(velocity.shape, jnp.float32)
    for moment in reversed(range(STEPS)):
        padded = adjoint_padded if moment == STEPS - 1 else padded_2(nearer, ((DEPTH, 1),), 4)
        laplacian = laplace(padded.astype(jnp.float32))
        updated = (
            2.0 * nearer.astype(jnp.float32) - farther.astype(jnp.float32) + wave_model * laplacian
        )
        updated = inject_rows(updated, receiver_cell, residuals[moment], anchor).astype(jnp.bfloat16)
        gradient = gradient + jnp.sum(
            updated.astype(jnp.float32) * images[moment].astype(jnp.float32), axis=0
        )
        farther, nearer = (nearer, updated)
    step_scale = step_base / math.sqrt(forward_start.shape[1] * lax.axis_size(SHOT))
    speed_rows = velocity.reshape(-1, velocity.shape[-1])

    def finish(summed, offset):
        speed = lax.dynamic_slice_in_dim(speed_rows, offset, summed.shape[0], 0)
        return jnp.clip(speed - step_scale * summed, low_speed, high_speed)

    velocity_new = reduce_shots(gradient, finish)
    forward_end = jnp.stack([earlier, current])
    adjoint_start = jnp.stack([nearer, farther])
    return (forward_end, adjoint_start, velocity_new)


def solution(mesh):
    fine = Mesh(mesh.devices.reshape(4, 4, 2, 4, 2), ("y", "zhi", "core", "x", "zlo"))
    placed = (
        P(None, SHOT, DEPTH, None, None),
        P(None, SHOT, DEPTH, None, None),
        P(DEPTH, None, None),
        P(SHOT),
        P(SHOT, None),
        P(SHOT, None),
        P(SHOT, None, None),
    )
    return jax.shard_map(
        body,
        mesh=fine,
        in_specs=placed,
        out_specs=(
            P(None, SHOT, DEPTH, None, None),
            P(None, SHOT, DEPTH, None, None),
            P(DEPTH, None, None),
        ),
        check_vma=False,
    )
```

```python
import math

import jax
import jax.numpy as jnp
from jax import lax
from jax.sharding import Mesh
from jax.sharding import PartitionSpec as P

SHOT = ("y", "zhi", "core")
DEPTH = ("x", "zlo")
CZ = 16
NX = 128
NY = 128
STEPS = 4


stencil_weights = (1.6, -0.2, 8.0 / 315.0, -1.0 / 560.0)
center_weight = -205.0 / 72.0
courant = 0.095
step_base = 0.01
low_speed = 1.5
high_speed = 4.5


def padded_2(cells, sides, width):
    for axis, dim in sides:
        count = lax.axis_size(axis)
        ends = count - 1
        head = lax.slice_in_dim(cells, 0, width, axis=dim)
        tail = lax.slice_in_dim(cells, cells.shape[dim] - width, cells.shape[dim], axis=dim)
        cells = jnp.concatenate(
            [
                lax.ppermute(tail, axis, [(i, (i + 1) % count) for i in range(ends)]),
                cells,
                lax.ppermute(head, axis, [((i + 1) % count, i) for i in range(ends)]),
            ],
            axis=dim,
        )
    return cells


def laplace(depth_padded):
    padded = jnp.pad(depth_padded, ((0, 0), (0, 0), (4, 4), (4, 4)))
    depth_len = padded.shape[1] - 8
    row_len = padded.shape[2] - 8
    column_len = padded.shape[3] - 8

    def window(along_z, along_x, along_y):
        return padded[
            :,
            4 + along_z : 4 + along_z + depth_len,
            4 + along_x : 4 + along_x + row_len,
            4 + along_y : 4 + along_y + column_len,
        ]

    summed = 3.0 * center_weight * window(0, 0, 0)
    for offset in range(1, 5):
        weight = stencil_weights[offset - 1]
        summed = summed + weight * (
            window(offset, 0, 0)
            + window(-offset, 0, 0)
            + window(0, offset, 0)
            + window(0, -offset, 0)
            + window(0, 0, offset)
            + window(0, 0, -offset)
        )
    return summed


def inject(wavefield, cell_ids, values, anchor):
    shot_count = wavefield.shape[0]
    depth_len = wavefield.shape[1]
    plane_size = NX * NY
    planes = cell_ids // plane_size - anchor
    owned_mask = (planes >= 0) & (planes < depth_len)
    flat_index = jnp.clip(planes, 0, depth_len - 1) * plane_size + cell_ids % plane_size
    rows_index = jnp.broadcast_to(jnp.arange(shot_count, dtype=jnp.int32)[:, None], cell_ids.shape)
    flattened = (
        wavefield.reshape(shot_count, -1)
        .at[rows_index, flat_index]
        .add(jnp.where(owned_mask, values, 0.0))
    )
    return flattened.reshape(wavefield.shape)


def cell_coords(cell_ids, anchor):
    plane_size = NX * NY
    planes = cell_ids // plane_size - anchor
    rest = cell_ids % plane_size
    return planes, rest // NY, rest % NY


def inject_one(wavefield, cell_ids, values, anchor):
    planes, rows, columns = cell_coords(cell_ids, anchor)
    shape = wavefield.shape
    hit = (
        (lax.broadcasted_iota(jnp.int32, shape, 1) == planes[:, None, None, None])
        & (lax.broadcasted_iota(jnp.int32, shape, 2) == rows[:, None, None, None])
        & (lax.broadcasted_iota(jnp.int32, shape, 3) == columns[:, None, None, None])
    )
    return jnp.where(hit, wavefield + values[:, :, None, None], wavefield)


def record_rows(wavefield, cell_ids, anchor):
    depth_len = wavefield.shape[1]
    planes, rows, columns = cell_coords(cell_ids, anchor)
    row_ids = jnp.clip(planes, 0, depth_len - 1) * NX + rows
    table = wavefield.reshape(-1, NY)
    choose = row_ids[0][:, None] == lax.broadcasted_iota(jnp.int32, (1, table.shape[0]), 1)
    picked = jnp.dot(choose.astype(table.dtype), table, preferred_element_type=jnp.float32)
    lanes = lax.broadcasted_iota(jnp.int32, picked.shape, 1)
    return jnp.sum(jnp.where(lanes == columns[0][:, None], picked, 0.0), axis=1)[None]


def inject_rows(wavefield, cell_ids, values, anchor):
    depth_len = wavefield.shape[1]
    planes, rows, columns = cell_coords(cell_ids, anchor)
    owned = (planes >= 0) & (planes < depth_len)
    row_ids = jnp.clip(planes, 0, depth_len - 1) * NX + rows
    count = depth_len * NX
    choose = row_ids[0][:, None] == lax.broadcasted_iota(jnp.int32, (1, count), 1)
    lanes = lax.broadcasted_iota(jnp.int32, (cell_ids.shape[1], NY), 1)
    spread = jnp.where(
        (lanes == columns[0][:, None]) & owned[0][:, None], values[0][:, None], 0.0
    )
    high = lax.reduce_precision(spread, exponent_bits=8, mantissa_bits=7)
    rest = spread - high
    middle = lax.reduce_precision(rest, exponent_bits=8, mantissa_bits=7)
    low = rest - middle
    pieces = jnp.concatenate([high, middle, low], axis=1).astype(jnp.bfloat16)
    parts = lax.dot_general(
        choose.astype(jnp.bfloat16),
        pieces,
        (((0,), (0,)), ((), ())),
        preferred_element_type=jnp.float32,
    )
    added = (parts[:, :NY] + parts[:, NY : 2 * NY]) + parts[:, 2 * NY :]
    return wavefield + added.reshape(wavefield.shape)


def record(wavefield, cell_ids, anchor):
    shot_count = wavefield.shape[0]
    plane_size = NX * NY
    planes = cell_ids // plane_size - anchor
    flat_index = jnp.clip(planes, 0, wavefield.shape[1] - 1) * plane_size + cell_ids % plane_size
    return jnp.take_along_axis(wavefield.reshape(shot_count, -1), flat_index, axis=1).astype(
        jnp.float32
    )


def reduce_shots(gradient, finish, riders):
    rows = gradient.reshape(-1, gradient.shape[-1])
    pair = [(0, 1), (1, 0)]
    bit = lax.axis_index("core")
    half = rows.shape[0] // 2
    keep = lax.dynamic_slice_in_dim(rows, bit * half, half, 0)
    send = lax.dynamic_slice_in_dim(rows, (1 - bit) * half, half, 0)
    rows = keep + lax.ppermute(send, "core", pair)
    rows, riders = lax.optimization_barrier((rows, riders))
    offset = bit * half
    for axis in ("y", "zhi"):
        count = lax.axis_size(axis)
        me = lax.axis_index(axis)
        part = rows.shape[0] // count
        kept = lax.dynamic_slice_in_dim(rows, me * part, part, 0)
        for shift in range(1, count):
            send = lax.dynamic_slice_in_dim(rows, ((me + shift) % count) * part, part, 0)
            kept = kept + lax.ppermute(send, axis, [(i, (i + shift) % count) for i in range(count)])
        rows = kept
        offset = offset + me * part
    rows = finish(rows, offset)
    for axis in ("zhi", "y"):
        count = lax.axis_size(axis)
        me = lax.axis_index(axis)
        part = rows.shape[0]
        whole = jnp.zeros((count * part, rows.shape[1]), rows.dtype)
        whole = lax.dynamic_update_slice_in_dim(whole, rows, me * part, 0)
        for shift in range(1, count):
            got = lax.ppermute(rows, axis, [(i, (i + shift) % count) for i in range(count)])
            whole = lax.dynamic_update_slice_in_dim(whole, got, ((me - shift) % count) * part, 0)
        rows = whole
    other = lax.ppermute(rows, "core", pair)
    rows = jnp.where(bit == 0, jnp.concatenate([rows, other]), jnp.concatenate([other, rows]))
    return rows.reshape(gradient.shape), riders


def body(forward_start, adjoint_end, velocity, source_cell, wavelet, receiver_cell, observed):
    anchor = lax.axis_index(DEPTH) * CZ
    wave_model = (courant * velocity) ** 2
    source_ids = source_cell[:, None]
    images = []
    residuals = []
    earlier = forward_start[0]
    current = forward_start[1]
    both = padded_2(jnp.concatenate([current, adjoint_end[0]]), ((DEPTH, 1),), 4)
    first_padded, adjoint_padded = both[:1], both[1:]
    for moment in range(STEPS):
        padded = first_padded if moment == 0 else padded_2(current, ((DEPTH, 1),), 4)
        laplacian = laplace(padded.astype(jnp.float32))
        updated = (
            2.0 * current.astype(jnp.float32) - earlier.astype(jnp.float32) + wave_model * laplacian
        )
        updated = inject_one(updated, source_cell, wavelet[:, moment : moment + 1], anchor).astype(
            jnp.bfloat16
        )
        images.append(laplacian.astype(jnp.bfloat16))
        residuals.append(record_rows(updated, receiver_cell, anchor) - observed[:, moment])
        earlier, current = (current, updated)
    images = list(lax.optimization_barrier(tuple(images)))
    nearer = adjoint_end[0]
    farther = adjoint_end[1]
    gradient = jnp.zeros(velocity.shape, jnp.float32)
    for moment in reversed(range(STEPS)):
        padded = adjoint_padded if moment == STEPS - 1 else padded_2(nearer, ((DEPTH, 1),), 4)
        laplacian = laplace(padded.astype(jnp.float32))
        updated = (
            2.0 * nearer.astype(jnp.float32) - farther.astype(jnp.float32) + wave_model * laplacian
        )
        updated = inject_rows(updated, receiver_cell, residuals[moment], anchor).astype(jnp.bfloat16)
        gradient = gradient + jnp.sum(
            updated.astype(jnp.float32) * images[moment].astype(jnp.float32), axis=0
        )
        farther, nearer = (nearer, updated)
    step_scale = step_base / math.sqrt(forward_start.shape[1] * lax.axis_size(SHOT))
    speed_rows = velocity.reshape(-1, velocity.shape[-1])

    def finish(summed, offset):
        speed = lax.dynamic_slice_in_dim(speed_rows, offset, summed.shape[0], 0)
        return jnp.clip(speed - step_scale * summed, low_speed, high_speed)

    velocity_new, (forward_end, adjoint_start) = reduce_shots(
        gradient, finish, (jnp.stack([earlier, current]), jnp.stack([nearer, farther]))
    )
    return (forward_end, adjoint_start, velocity_new)


def solution(mesh):
    fine = Mesh(mesh.devices.reshape(4, 4, 2, 4, 2), ("y", "zhi", "core", "x", "zlo"))
    placed = (
        P(None, SHOT, DEPTH, None, None),
        P(None, SHOT, DEPTH, None, None),
        P(DEPTH, None, None),
        P(SHOT),
        P(SHOT, None),
        P(SHOT, None),
        P(SHOT, None, None),
    )
    return jax.shard_map(
        body,
        mesh=fine,
        in_specs=placed,
        out_specs=(
            P(None, SHOT, DEPTH, None, None),
            P(None, SHOT, DEPTH, None, None),
            P(DEPTH, None, None),
        ),
        check_vma=False,
    )
```

```python
import math

import jax
import jax.numpy as jnp
from jax import lax
from jax.sharding import Mesh
from jax.sharding import PartitionSpec as P

SHOT = ("y", "zhi", "core")
DEPTH = ("x", "zlo")
CZ = 16
NX = 128
NY = 128
STEPS = 4


stencil_weights = (1.6, -0.2, 8.0 / 315.0, -1.0 / 560.0)
center_weight = -205.0 / 72.0
courant = 0.095
step_base = 0.01
low_speed = 1.5
high_speed = 4.5


def padded_2(cells, sides, width):
    for axis, dim in sides:
        count = lax.axis_size(axis)
        ends = count - 1
        head = lax.slice_in_dim(cells, 0, width, axis=dim)
        tail = lax.slice_in_dim(cells, cells.shape[dim] - width, cells.shape[dim], axis=dim)
        cells = jnp.concatenate(
            [
                lax.ppermute(tail, axis, [(i, (i + 1) % count) for i in range(ends)]),
                cells,
                lax.ppermute(head, axis, [((i + 1) % count, i) for i in range(ends)]),
            ],
            axis=dim,
        )
    return cells


def laplace(depth_padded):
    padded = jnp.pad(depth_padded, ((0, 0), (0, 0), (4, 4), (4, 4)))
    depth_len = padded.shape[1] - 8
    row_len = padded.shape[2] - 8
    column_len = padded.shape[3] - 8

    def window(along_z, along_x, along_y):
        return padded[
            :,
            4 + along_z : 4 + along_z + depth_len,
            4 + along_x : 4 + along_x + row_len,
            4 + along_y : 4 + along_y + column_len,
        ]

    summed = 3.0 * center_weight * window(0, 0, 0)
    for offset in range(1, 5):
        weight = stencil_weights[offset - 1]
        summed = summed + weight * (
            window(offset, 0, 0)
            + window(-offset, 0, 0)
            + window(0, offset, 0)
            + window(0, -offset, 0)
            + window(0, 0, offset)
            + window(0, 0, -offset)
        )
    return summed


def inject(wavefield, cell_ids, values, anchor):
    shot_count = wavefield.shape[0]
    depth_len = wavefield.shape[1]
    plane_size = NX * NY
    planes = cell_ids // plane_size - anchor
    owned_mask = (planes >= 0) & (planes < depth_len)
    flat_index = jnp.clip(planes, 0, depth_len - 1) * plane_size + cell_ids % plane_size
    rows_index = jnp.broadcast_to(jnp.arange(shot_count, dtype=jnp.int32)[:, None], cell_ids.shape)
    flattened = (
        wavefield.reshape(shot_count, -1)
        .at[rows_index, flat_index]
        .add(jnp.where(owned_mask, values, 0.0))
    )
    return flattened.reshape(wavefield.shape)


def cell_coords(cell_ids, anchor):
    plane_size = NX * NY
    planes = cell_ids // plane_size - anchor
    rest = cell_ids % plane_size
    return planes, rest // NY, rest % NY


def inject_one(wavefield, cell_ids, values, anchor):
    planes, rows, columns = cell_coords(cell_ids, anchor)
    shape = wavefield.shape
    hit = (
        (lax.broadcasted_iota(jnp.int32, shape, 1) == planes[:, None, None, None])
        & (lax.broadcasted_iota(jnp.int32, shape, 2) == rows[:, None, None, None])
        & (lax.broadcasted_iota(jnp.int32, shape, 3) == columns[:, None, None, None])
    )
    return jnp.where(hit, wavefield + values[:, :, None, None], wavefield)


def record_rows(wavefield, cell_ids, anchor):
    depth_len = wavefield.shape[1]
    planes, rows, columns = cell_coords(cell_ids, anchor)
    row_ids = jnp.clip(planes, 0, depth_len - 1) * NX + rows
    table = wavefield.reshape(-1, NY)
    choose = row_ids[0][:, None] == lax.broadcasted_iota(jnp.int32, (1, table.shape[0]), 1)
    picked = jnp.dot(choose.astype(table.dtype), table, preferred_element_type=jnp.float32)
    lanes = lax.broadcasted_iota(jnp.int32, picked.shape, 1)
    return jnp.sum(jnp.where(lanes == columns[0][:, None], picked, 0.0), axis=1)[None]


def inject_rows(wavefield, cell_ids, values, anchor):
    depth_len = wavefield.shape[1]
    planes, rows, columns = cell_coords(cell_ids, anchor)
    owned = (planes >= 0) & (planes < depth_len)
    row_ids = jnp.clip(planes, 0, depth_len - 1) * NX + rows
    count = depth_len * NX
    choose = row_ids[0][:, None] == lax.broadcasted_iota(jnp.int32, (1, count), 1)
    lanes = lax.broadcasted_iota(jnp.int32, (cell_ids.shape[1], NY), 1)
    spread = jnp.where(
        (lanes == columns[0][:, None]) & owned[0][:, None], values[0][:, None], 0.0
    )
    high = lax.reduce_precision(spread, exponent_bits=8, mantissa_bits=7)
    rest = spread - high
    middle = lax.reduce_precision(rest, exponent_bits=8, mantissa_bits=7)
    low = rest - middle
    pieces = jnp.concatenate([high, middle, low], axis=1).astype(jnp.bfloat16)
    parts = lax.dot_general(
        choose.astype(jnp.bfloat16),
        pieces,
        (((0,), (0,)), ((), ())),
        preferred_element_type=jnp.float32,
    )
    added = (parts[:, :NY] + parts[:, NY : 2 * NY]) + parts[:, 2 * NY :]
    return wavefield + added.reshape(wavefield.shape)


def record(wavefield, cell_ids, anchor):
    shot_count = wavefield.shape[0]
    plane_size = NX * NY
    planes = cell_ids // plane_size - anchor
    flat_index = jnp.clip(planes, 0, wavefield.shape[1] - 1) * plane_size + cell_ids % plane_size
    return jnp.take_along_axis(wavefield.reshape(shot_count, -1), flat_index, axis=1).astype(
        jnp.float32
    )


def reduce_shots(gradient, finish):
    rows = gradient.reshape(-1, gradient.shape[-1])
    pair = [(0, 1), (1, 0)]
    bit = lax.axis_index("core")
    half = rows.shape[0] // 2
    keep = lax.dynamic_slice_in_dim(rows, bit * half, half, 0)
    send = lax.dynamic_slice_in_dim(rows, (1 - bit) * half, half, 0)
    rows = keep + lax.ppermute(send, "core", pair)
    offset = bit * half
    for axis in ("y", "zhi"):
        count = lax.axis_size(axis)
        me = lax.axis_index(axis)
        part = rows.shape[0] // count
        kept = lax.dynamic_slice_in_dim(rows, me * part, part, 0)
        for shift in range(1, count):
            send = lax.dynamic_slice_in_dim(rows, ((me + shift) % count) * part, part, 0)
            kept = kept + lax.ppermute(send, axis, [(i, (i + shift) % count) for i in range(count)])
        rows = kept
        offset = offset + me * part
    rows = finish(rows, offset)
    for axis in ("zhi", "y"):
        count = lax.axis_size(axis)
        me = lax.axis_index(axis)
        part = rows.shape[0]
        whole = jnp.zeros((count * part, rows.shape[1]), rows.dtype)
        whole = lax.dynamic_update_slice_in_dim(whole, rows, me * part, 0)
        for shift in range(1, count):
            got = lax.ppermute(rows, axis, [(i, (i + shift) % count) for i in range(count)])
            whole = lax.dynamic_update_slice_in_dim(whole, got, ((me - shift) % count) * part, 0)
        rows = whole
    other = lax.ppermute(rows, "core", pair)
    rows = jnp.where(bit == 0, jnp.concatenate([rows, other]), jnp.concatenate([other, rows]))
    return rows.reshape(gradient.shape)


def body(forward_start, adjoint_end, velocity, source_cell, wavelet, receiver_cell, observed):
    anchor = lax.axis_index(DEPTH) * CZ
    wave_model = (courant * velocity) ** 2
    source_ids = source_cell[:, None]
    images = []
    residuals = []
    earlier = forward_start[0]
    current = forward_start[1]
    both = padded_2(jnp.concatenate([current, adjoint_end[0]]), ((DEPTH, 1),), 4)
    first_padded, adjoint_padded = both[:1], both[1:]
    nearer = adjoint_end[0]
    farther = adjoint_end[1]
    early = (
        2.0 * nearer.astype(jnp.float32)
        - farther.astype(jnp.float32)
        + wave_model * laplace(adjoint_padded.astype(jnp.float32))
    )
    for moment in range(STEPS):
        padded = first_padded if moment == 0 else padded_2(current, ((DEPTH, 1),), 4)
        if moment == 1:
            padded, early = lax.optimization_barrier((padded, early))
        laplacian = laplace(padded.astype(jnp.float32))
        updated = (
            2.0 * current.astype(jnp.float32) - earlier.astype(jnp.float32) + wave_model * laplacian
        )
        updated = inject_one(updated, source_cell, wavelet[:, moment : moment + 1], anchor).astype(
            jnp.bfloat16
        )
        images.append(laplacian.astype(jnp.bfloat16))
        residuals.append(record_rows(updated, receiver_cell, anchor) - observed[:, moment])
        earlier, current = (current, updated)
    images = list(lax.optimization_barrier(tuple(images)))
    nearer = adjoint_end[0]
    farther = adjoint_end[1]
    gradient = jnp.zeros(velocity.shape, jnp.float32)
    for moment in reversed(range(STEPS)):
        if moment == STEPS - 1:
            updated = early
        else:
            padded = padded_2(nearer, ((DEPTH, 1),), 4)
            laplacian = laplace(padded.astype(jnp.float32))
            updated = (
                2.0 * nearer.astype(jnp.float32)
                - farther.astype(jnp.float32)
                + wave_model * laplacian
            )
        updated = inject_rows(updated, receiver_cell, residuals[moment], anchor).astype(jnp.bfloat16)
        gradient = gradient + jnp.sum(
            updated.astype(jnp.float32) * images[moment].astype(jnp.float32), axis=0
        )
        farther, nearer = (nearer, updated)
    step_scale = step_base / math.sqrt(forward_start.shape[1] * lax.axis_size(SHOT))
    speed_rows = velocity.reshape(-1, velocity.shape[-1])

    def finish(summed, offset):
        speed = lax.dynamic_slice_in_dim(speed_rows, offset, summed.shape[0], 0)
        return jnp.clip(speed - step_scale * summed, low_speed, high_speed)

    velocity_new = reduce_shots(gradient, finish)
    forward_end = jnp.stack([earlier, current])
    adjoint_start = jnp.stack([nearer, farther])
    return (forward_end, adjoint_start, velocity_new)


def solution(mesh):
    fine = Mesh(mesh.devices.reshape(4, 4, 2, 4, 2), ("y", "zhi", "core", "x", "zlo"))
    placed = (
        P(None, SHOT, DEPTH, None, None),
        P(None, SHOT, DEPTH, None, None),
        P(DEPTH, None, None),
        P(SHOT),
        P(SHOT, None),
        P(SHOT, None),
        P(SHOT, None, None),
    )
    return jax.shard_map(
        body,
        mesh=fine,
        in_specs=placed,
        out_specs=(
            P(None, SHOT, DEPTH, None, None),
            P(None, SHOT, DEPTH, None, None),
            P(DEPTH, None, None),
        ),
        check_vma=False,
    )
```

```python
import math

import jax
import jax.numpy as jnp
from jax import lax
from jax.sharding import Mesh
from jax.sharding import PartitionSpec as P

SHOT = ("y", "zhi", "core")
DEPTH = ("x", "zlo")
CZ = 16
NX = 128
NY = 128
STEPS = 4


stencil_weights = (1.6, -0.2, 8.0 / 315.0, -1.0 / 560.0)
center_weight = -205.0 / 72.0
courant = 0.095
step_base = 0.01
low_speed = 1.5
high_speed = 4.5


def padded_2(cells, sides, width):
    for axis, dim in sides:
        count = lax.axis_size(axis)
        ends = count - 1
        head = lax.slice_in_dim(cells, 0, width, axis=dim)
        tail = lax.slice_in_dim(cells, cells.shape[dim] - width, cells.shape[dim], axis=dim)
        cells = jnp.concatenate(
            [
                lax.ppermute(tail, axis, [(i, (i + 1) % count) for i in range(ends)]),
                cells,
                lax.ppermute(head, axis, [((i + 1) % count, i) for i in range(ends)]),
            ],
            axis=dim,
        )
    return cells


def laplace(depth_padded):
    padded = jnp.pad(depth_padded, ((0, 0), (0, 0), (4, 4), (4, 4)))
    depth_len = padded.shape[1] - 8
    row_len = padded.shape[2] - 8
    column_len = padded.shape[3] - 8

    def window(along_z, along_x, along_y):
        return padded[
            :,
            4 + along_z : 4 + along_z + depth_len,
            4 + along_x : 4 + along_x + row_len,
            4 + along_y : 4 + along_y + column_len,
        ]

    summed = 3.0 * center_weight * window(0, 0, 0)
    for offset in range(1, 5):
        weight = stencil_weights[offset - 1]
        summed = summed + weight * (
            window(offset, 0, 0)
            + window(-offset, 0, 0)
            + window(0, offset, 0)
            + window(0, -offset, 0)
            + window(0, 0, offset)
            + window(0, 0, -offset)
        )
    return summed


def inject(wavefield, cell_ids, values, anchor):
    shot_count = wavefield.shape[0]
    depth_len = wavefield.shape[1]
    plane_size = NX * NY
    planes = cell_ids // plane_size - anchor
    owned_mask = (planes >= 0) & (planes < depth_len)
    flat_index = jnp.clip(planes, 0, depth_len - 1) * plane_size + cell_ids % plane_size
    rows_index = jnp.broadcast_to(jnp.arange(shot_count, dtype=jnp.int32)[:, None], cell_ids.shape)
    flattened = (
        wavefield.reshape(shot_count, -1)
        .at[rows_index, flat_index]
        .add(jnp.where(owned_mask, values, 0.0))
    )
    return flattened.reshape(wavefield.shape)


def cell_coords(cell_ids, anchor):
    plane_size = NX * NY
    planes = cell_ids // plane_size - anchor
    rest = cell_ids % plane_size
    return planes, rest // NY, rest % NY


def inject_one(wavefield, cell_ids, values, anchor):
    planes, rows, columns = cell_coords(cell_ids, anchor)
    shape = wavefield.shape
    hit = (
        (lax.broadcasted_iota(jnp.int32, shape, 1) == planes[:, None, None, None])
        & (lax.broadcasted_iota(jnp.int32, shape, 2) == rows[:, None, None, None])
        & (lax.broadcasted_iota(jnp.int32, shape, 3) == columns[:, None, None, None])
    )
    return jnp.where(hit, wavefield + values[:, :, None, None], wavefield)


def record_rows(wavefield, cell_ids, anchor):
    depth_len = wavefield.shape[1]
    planes, rows, columns = cell_coords(cell_ids, anchor)
    row_ids = jnp.clip(planes, 0, depth_len - 1) * NX + rows
    table = wavefield.reshape(-1, NY)
    choose = row_ids[0][:, None] == lax.broadcasted_iota(jnp.int32, (1, table.shape[0]), 1)
    picked = jnp.dot(choose.astype(table.dtype), table, preferred_element_type=jnp.float32)
    lanes = lax.broadcasted_iota(jnp.int32, picked.shape, 1)
    return jnp.sum(jnp.where(lanes == columns[0][:, None], picked, 0.0), axis=1)[None]


def inject_rows(wavefield, cell_ids, values, anchor):
    depth_len = wavefield.shape[1]
    planes, rows, columns = cell_coords(cell_ids, anchor)
    owned = (planes >= 0) & (planes < depth_len)
    row_ids = jnp.clip(planes, 0, depth_len - 1) * NX + rows
    count = depth_len * NX
    choose = row_ids[0][:, None] == lax.broadcasted_iota(jnp.int32, (1, count), 1)
    lanes = lax.broadcasted_iota(jnp.int32, (cell_ids.shape[1], NY), 1)
    spread = jnp.where(
        (lanes == columns[0][:, None]) & owned[0][:, None], values[0][:, None], 0.0
    )
    high = lax.reduce_precision(spread, exponent_bits=8, mantissa_bits=7)
    rest = spread - high
    middle = lax.reduce_precision(rest, exponent_bits=8, mantissa_bits=7)
    low = rest - middle
    pieces = jnp.concatenate([high, middle, low], axis=1).astype(jnp.bfloat16)
    parts = lax.dot_general(
        choose.astype(jnp.bfloat16),
        pieces,
        (((0,), (0,)), ((), ())),
        preferred_element_type=jnp.float32,
    )
    added = (parts[:, :NY] + parts[:, NY : 2 * NY]) + parts[:, 2 * NY :]
    return wavefield + added.reshape(wavefield.shape)


def record(wavefield, cell_ids, anchor):
    shot_count = wavefield.shape[0]
    plane_size = NX * NY
    planes = cell_ids // plane_size - anchor
    flat_index = jnp.clip(planes, 0, wavefield.shape[1] - 1) * plane_size + cell_ids % plane_size
    return jnp.take_along_axis(wavefield.reshape(shot_count, -1), flat_index, axis=1).astype(
        jnp.float32
    )


def reduce_shots(gradient, finish, riders):
    rows = gradient.reshape(-1, gradient.shape[-1])
    pair = [(0, 1), (1, 0)]
    bit = lax.axis_index("core")
    half = rows.shape[0] // 2
    keep = lax.dynamic_slice_in_dim(rows, bit * half, half, 0)
    send = lax.dynamic_slice_in_dim(rows, (1 - bit) * half, half, 0)
    rows = keep + lax.ppermute(send, "core", pair)
    rows, riders = lax.optimization_barrier((rows, riders))
    offset = bit * half
    for axis in ("y", "zhi"):
        count = lax.axis_size(axis)
        me = lax.axis_index(axis)
        part = rows.shape[0] // count
        kept = lax.dynamic_slice_in_dim(rows, me * part, part, 0)
        for shift in range(1, count):
            send = lax.dynamic_slice_in_dim(rows, ((me + shift) % count) * part, part, 0)
            kept = kept + lax.ppermute(send, axis, [(i, (i + shift) % count) for i in range(count)])
        rows = kept
        offset = offset + me * part
    rows = finish(rows, offset)
    for axis in ("zhi", "y"):
        count = lax.axis_size(axis)
        me = lax.axis_index(axis)
        part = rows.shape[0]
        whole = jnp.zeros((count * part, rows.shape[1]), rows.dtype)
        whole = lax.dynamic_update_slice_in_dim(whole, rows, me * part, 0)
        for shift in range(1, count):
            got = lax.ppermute(rows, axis, [(i, (i + shift) % count) for i in range(count)])
            whole = lax.dynamic_update_slice_in_dim(whole, got, ((me - shift) % count) * part, 0)
        rows = whole
    other = lax.ppermute(rows, "core", pair)
    whole = jnp.zeros((2 * rows.shape[0], rows.shape[1]), rows.dtype)
    whole = lax.dynamic_update_slice_in_dim(whole, rows, bit * rows.shape[0], 0)
    whole = lax.dynamic_update_slice_in_dim(whole, other, (1 - bit) * rows.shape[0], 0)
    return whole.reshape(gradient.shape), riders


def body(forward_start, adjoint_end, velocity, source_cell, wavelet, receiver_cell, observed):
    anchor = lax.axis_index(DEPTH) * CZ
    wave_model = (courant * velocity) ** 2
    source_ids = source_cell[:, None]
    images = []
    residuals = []
    earlier = forward_start[0]
    current = forward_start[1]
    both = padded_2(jnp.concatenate([current, adjoint_end[0]]), ((DEPTH, 1),), 4)
    first_padded, adjoint_padded = both[:1], both[1:]
    nearer = adjoint_end[0]
    farther = adjoint_end[1]
    early = (
        2.0 * nearer.astype(jnp.float32)
        - farther.astype(jnp.float32)
        + wave_model * laplace(adjoint_padded.astype(jnp.float32))
    )
    for moment in range(STEPS):
        padded = first_padded if moment == 0 else padded_2(current, ((DEPTH, 1),), 4)
        if moment == 1:
            padded, early = lax.optimization_barrier((padded, early))
        laplacian = laplace(padded.astype(jnp.float32))
        updated = (
            2.0 * current.astype(jnp.float32) - earlier.astype(jnp.float32) + wave_model * laplacian
        )
        updated = inject_one(updated, source_cell, wavelet[:, moment : moment + 1], anchor).astype(
            jnp.bfloat16
        )
        images.append(laplacian.astype(jnp.bfloat16))
        residuals.append(record_rows(updated, receiver_cell, anchor) - observed[:, moment])
        earlier, current = (current, updated)
    images = list(lax.optimization_barrier(tuple(images)))
    nearer = adjoint_end[0]
    farther = adjoint_end[1]
    gradient = jnp.zeros(velocity.shape, jnp.float32)
    for moment in reversed(range(STEPS)):
        if moment == STEPS - 1:
            updated = early
        else:
            padded = padded_2(nearer, ((DEPTH, 1),), 4)
            laplacian = laplace(padded.astype(jnp.float32))
            updated = (
                2.0 * nearer.astype(jnp.float32)
                - farther.astype(jnp.float32)
                + wave_model * laplacian
            )
        updated = inject_rows(updated, receiver_cell, residuals[moment], anchor).astype(jnp.bfloat16)
        gradient = gradient + jnp.sum(
            updated.astype(jnp.float32) * images[moment].astype(jnp.float32), axis=0
        )
        farther, nearer = (nearer, updated)
    step_scale = step_base / math.sqrt(forward_start.shape[1] * lax.axis_size(SHOT))
    speed_rows = velocity.reshape(-1, velocity.shape[-1])

    def finish(summed, offset):
        speed = lax.dynamic_slice_in_dim(speed_rows, offset, summed.shape[0], 0)
        return jnp.clip(speed - step_scale * summed, low_speed, high_speed)

    velocity_new, (forward_end, adjoint_start) = reduce_shots(
        gradient, finish, (jnp.stack([earlier, current]), jnp.stack([nearer, farther]))
    )
    return (forward_end, adjoint_start, velocity_new)


def solution(mesh):
    fine = Mesh(mesh.devices.reshape(4, 4, 2, 4, 2), ("y", "zhi", "core", "x", "zlo"))
    placed = (
        P(None, SHOT, DEPTH, None, None),
        P(None, SHOT, DEPTH, None, None),
        P(DEPTH, None, None),
        P(SHOT),
        P(SHOT, None),
        P(SHOT, None),
        P(SHOT, None, None),
    )
    return jax.shard_map(
        body,
        mesh=fine,
        in_specs=placed,
        out_specs=(
            P(None, SHOT, DEPTH, None, None),
            P(None, SHOT, DEPTH, None, None),
            P(DEPTH, None, None),
        ),
        check_vma=False,
    )
```
